32 devices in a mesh: dp: 4 (over z), vocab: 8 (over y, x, core).
Axes of the slice: x: 2, y: 2, z: 4, core: 2. Of those that a mesh axis runs over, the one named last changes fastest.
Arguments:
- hidden: bfloat16 [512, 8192], P('dp', 'vocab'), may hold values from -8 to 8
- out_weight: bfloat16 [19456, 8192], P('vocab', 'dp'), may hold values from -0.397747564 to 0.397747564
- token_blocks: int32 [8, 4, 16], P('vocab'), may hold values from 0 to 18, as said below
- counts: int32 [8, 4], P('vocab'), may hold values from 4 to 16, as said below
Outputs:
- allowed_logprob: float32 [8, 4, 16, 128, 128], P('vocab', 'dp')
- expected: float32 [512, 8192], P('vocab', 'dp')
The draws below stay inside these ranges and needn't reach their ends.
Inputs may be any that keep to these rules, and one draw needn't show every extreme that they name: token_blocks[j, b, s] names one of the 19 token blocks of shard j; the entries of one list are distinct; slots at or past counts[j, b] carry no meaning. `counts`: for every beam block, some shard allows exactly 16 slots.
All inputs are finite; a program needn't handle non-finite values.
Results may differ from the reference program's by a relative error of at most 0.0021.
Values may be sent and summed in bfloat16 or wider, within the bound.
No kernel may reach another device: no remote copies, remote signals or barrier semaphores. Data moves between devices by JAX's collectives and lax.ppermute only.
A program may use at most 128 MiB of HBM per device.

```python
import math
import jax
import jax.numpy as jnp
from jax import lax

D = 8192
VB_DEV = 19
TB = 128
BB = 128
MOST = 16
NBLK = 4
BEAMS = 512
VOCAB = 19456
N_VOCAB = 8


def draw_lists(key):
    base_key = jax.random.fold_in(key, 11)
    keys_all = jax.random.split(base_key, 5)
    ceilings = jax.random.randint(keys_all[0], (N_VOCAB, 1), max(MOST // 2, 1), MOST + 1)
    lowest = jnp.maximum(ceilings // 2, 1)
    allowed = jax.random.randint(keys_all[1], (N_VOCAB, NBLK), lowest, ceilings + 1)
    full_shard = jax.random.randint(keys_all[2], (NBLK,), 0, N_VOCAB)
    low_shard = (full_shard + jax.random.randint(keys_all[4], (NBLK,), 1, N_VOCAB)) % N_VOCAB
    shard_range = jnp.arange(N_VOCAB)[:, None]
    allowed = jnp.where(shard_range == low_shard[None, :], max(MOST // 4, 1), allowed)
    allowed = jnp.where(shard_range == full_shard[None, :], MOST, allowed)
    scores = jax.random.randint(keys_all[3], (N_VOCAB, NBLK, VB_DEV), 0, 1048576) * VB_DEV + jnp.arange(VB_DEV)
    ordering = jnp.argsort(scores, axis=-1)
    return (ordering[:, :, :MOST].astype(jnp.int32), allowed.astype(jnp.int32))


def draw_token_blocks(key, part):
    return draw_lists(key)[0]


def draw_counts(key, part):
    return draw_lists(key)[1]


def draw_hidden(key, part):
    values = jnp.clip(jax.random.normal(jax.random.fold_in(key, 1), (BEAMS, D), jnp.float32), -6.0, 6.0)
    return values.astype(jnp.bfloat16)


def draw_out_weight(key, part):
    base = jnp.clip(jax.random.normal(jax.random.fold_in(key, 5), (VOCAB, D), jnp.float32), -4.0, 4.0)
    ramp = 3.0 ** (jnp.arange(D, dtype=jnp.float32) / (D - 1) - 0.5)
    jitter = jnp.exp(jax.random.uniform(jax.random.fold_in(key, 6), (D,), jnp.float32, -0.8, 0.8))
    values = base * (ramp * jitter)[None, :] * (3.0 / math.sqrt(1.8 * D))
    return values.astype(jnp.bfloat16)


def setup_inputs(seed: int = 0) -> dict:
    keys = jax.random.split(jax.random.key(seed), 5)
    hidden = draw_hidden(jax.random.fold_in(keys[4], 71), 0)
    out_weight = draw_out_weight(jax.random.fold_in(keys[4], 71), 0)
    token_blocks = draw_token_blocks(jax.random.fold_in(keys[4], 71), 0)
    counts = draw_counts(jax.random.fold_in(keys[4], 71), 0)
    return dict(hidden=hidden, out_weight=out_weight, token_blocks=token_blocks, counts=counts)


def reference(hidden, out_weight, token_blocks, counts):
    weight_blocks = out_weight.reshape(N_VOCAB, VB_DEV, TB, D)
    beam_blocks = hidden.reshape(NBLK, BB, D)
    block_range = jnp.arange(NBLK, dtype=jnp.int32)

    def shard_logits(shard_index):
        shard_rows = weight_blocks[shard_index]

        def block_logits(block_index):
            picked = shard_rows[token_blocks[shard_index, block_index]].astype(jnp.float32)
            return jnp.einsum('rd,std->srt', beam_blocks[block_index].astype(jnp.float32), picked)
        return lax.map(block_logits, block_range)
    logits = lax.map(shard_logits, jnp.arange(N_VOCAB, dtype=jnp.int32))
    live = jnp.arange(MOST, dtype=jnp.int32)[None, None, :] < counts[:, :, None]
    live_mask = live[:, :, :, None, None]
    masked = jnp.where(live_mask, logits, -jnp.inf)
    beam_max = lax.optimization_barrier(jnp.max(masked, axis=(0, 2, 4)))
    centred = masked - beam_max[None, :, None, :, None]
    beam_total = lax.optimization_barrier(jnp.sum(jnp.exp(centred), axis=(0, 2, 4)))
    shifted = centred - jnp.log(beam_total)[None, :, None, :, None]
    allowed_logprob = jnp.where(live_mask, shifted, 0.0)
    probs = jnp.where(live_mask, jnp.exp(shifted), 0.0).astype(jnp.bfloat16)

    def add_shard(shard_index, running):
        shard_rows = weight_blocks[shard_index]
        shard_probs = probs[shard_index]

        def block_terms(block_index):
            picked = shard_rows[token_blocks[shard_index, block_index]].astype(jnp.float32)
            return jnp.einsum('srt,std->rd', shard_probs[block_index].astype(jnp.float32), picked)
        return running + lax.map(block_terms, block_range)
    summed = lax.fori_loop(0, N_VOCAB, add_shard, jnp.zeros((NBLK, BB, D), jnp.float32)).reshape(BEAMS, D)
    meansq = lax.optimization_barrier(jnp.mean(summed * summed, axis=1, keepdims=True))
    expected = summed / jnp.sqrt(meansq + 1e-06)
    return (allowed_logprob, expected)
```

```python
import jax
import jax.numpy as jnp
from jax import lax
from jax.sharding import PartitionSpec as P

TB = 128
BB = 128
MOST = 16


def per_device(hidden, out_weight, token_blocks, counts):
    vocab_here, columns_here = out_weight.shape
    width = hidden.shape[1] * lax.psum(1, "vocab")
    n_tb = vocab_here // TB
    block_lists = token_blocks[0]
    block_counts = counts[0]
    n_blk = block_lists.shape[0]
    own_blocks = hidden.shape[0] // BB
    first_block = lax.axis_index("dp") * own_blocks
    own_counts = lax.dynamic_slice_in_dim(block_counts, first_block, own_blocks, 0)

    beam_rows = lax.all_gather(hidden, "vocab", axis=1, tiled=True)
    beam_columns = lax.all_to_all(beam_rows, "dp", split_axis=1, concat_axis=0, tiled=True)

    with jax.named_scope("dense_logits"):
        full = jnp.einsum(
            "bd,vd->bv", beam_columns, out_weight, preferred_element_type=jnp.float32
        )
        full4 = full.reshape(n_blk, BB, n_tb, TB)
        rows = jnp.arange(n_blk, dtype=jnp.int32)[:, None]
        picked = full4[rows, :, block_lists, :]

    logits = lax.psum_scatter(picked, "dp", scatter_dimension=0, tiled=True)

    with jax.named_scope("softmax_stats"):
        live = jnp.arange(MOST, dtype=jnp.int32)[None, :] < own_counts[:, None]
        live_mask = live[:, :, None, None]
        masked = jnp.where(live_mask, logits, -jnp.inf)
        local_max = jnp.max(masked, axis=(1, 3))
        local_total = jnp.sum(jnp.exp(masked - local_max[:, None, :, None]), axis=(1, 3))
        stats = lax.all_gather(jnp.stack([local_max, local_total]), "vocab", axis=0)
        beam_max = jnp.max(stats[:, 0], axis=0)
        beam_total = jnp.sum(stats[:, 1] * jnp.exp(stats[:, 0] - beam_max[None]), axis=0)
        shifted = logits - beam_max[:, None, :, None] - jnp.log(beam_total)[:, None, :, None]
        allowed_logprob = jnp.where(live_mask, shifted, 0.0)
        probabilities = jnp.where(live_mask, jnp.exp(shifted), 0.0).astype(jnp.bfloat16)

    prob_part = lax.all_gather(probabilities, "dp", axis=0, tiled=True)

    with jax.named_scope("dense_expected"):
        onehot = (
            block_lists[:, :, None] == jnp.arange(n_tb, dtype=jnp.int32)[None, None, :]
        ).astype(jnp.bfloat16)
        spread = jnp.einsum(
            "bsk,bsrt->brkt", onehot, prob_part, preferred_element_type=jnp.float32
        ).astype(jnp.bfloat16)
        embedding_part = jnp.einsum(
            "bv,vd->bd",
            spread.reshape(n_blk * BB, n_tb * TB),
            out_weight,
            preferred_element_type=jnp.float32,
        )
    summed = lax.psum_scatter(embedding_part, "vocab", scatter_dimension=0, tiled=True)
    squares = lax.psum(jnp.sum(summed * summed, axis=1), "dp")
    expected = summed * lax.rsqrt(squares / width + 1e-06)[:, None]
    return (allowed_logprob[None], expected)


def solution(mesh):
    in_specs = (P("dp", "vocab"), P("vocab", "dp"), P("vocab", None, None), P("vocab", None))
    out_specs = (P("vocab", "dp", None, None, None), P("vocab", "dp"))
    return jax.shard_map(
        per_device, mesh=mesh, in_specs=in_specs, out_specs=out_specs, check_vma=False
    )
```

```python
import jax
import jax.numpy as jnp
from jax import lax
from jax.sharding import PartitionSpec as P

TB = 128
BB = 128
MOST = 16


def per_device(hidden, out_weight, token_blocks, counts):
    vocab_here, columns_here = out_weight.shape
    n_tb = vocab_here // TB
    block_lists = token_blocks[0]
    block_counts = counts[0]
    n_blk = block_lists.shape[0]
    own_blocks = hidden.shape[0] // BB
    first_block = lax.axis_index("dp") * own_blocks
    own_counts = lax.dynamic_slice_in_dim(block_counts, first_block, own_blocks, 0)

    n_vocab = lax.psum(1, "vocab")
    n_dp = lax.psum(1, "dp")
    with jax.named_scope("hidden_spread"):
        row_slices = lax.all_to_all(hidden, "vocab", split_axis=0, concat_axis=1, tiled=True)
        plane_rows = lax.all_to_all(row_slices, "dp", split_axis=1, concat_axis=0, tiled=True)
        gathered = lax.all_gather(plane_rows, "vocab", axis=0, tiled=True)
        group = hidden.shape[0] // n_vocab
        beam_columns = (
            gathered.reshape(n_vocab, n_dp, group, columns_here)
            .transpose(1, 0, 2, 3)
            .reshape(n_dp * n_vocab * group, columns_here)
        )

    with jax.named_scope("dense_logits"):
        full = jnp.einsum(
            "bd,vd->bv", beam_columns, out_weight, preferred_element_type=jnp.float32
        )
        full4 = full.reshape(n_blk, BB, n_tb, TB)
        rows = jnp.arange(n_blk, dtype=jnp.int32)[:, None]
        picked = full4[rows, :, block_lists, :]

    logits = lax.psum_scatter(picked, "dp", scatter_dimension=0, tiled=True)

    with jax.named_scope("softmax_stats"):
        live = jnp.arange(MOST, dtype=jnp.int32)[None, :] < own_counts[:, None]
        live_mask = live[:, :, None, None]
        masked = jnp.where(live_mask, logits, -jnp.inf)
        local_max = jnp.max(masked, axis=(1, 3))
        local_total = jnp.sum(jnp.exp(masked - local_max[:, None, :, None]), axis=(1, 3))
        stats = lax.all_gather(jnp.stack([local_max, local_total]), "vocab", axis=0)
        beam_max = jnp.max(stats[:, 0], axis=0)
        beam_total = jnp.sum(stats[:, 1] * jnp.exp(stats[:, 0] - beam_max[None]), axis=0)
        shifted = logits - beam_max[:, None, :, None] - jnp.log(beam_total)[:, None, :, None]
        allowed_logprob = jnp.where(live_mask, shifted, 0.0)
        probabilities = jnp.where(live_mask, jnp.exp(shifted), 0.0).astype(jnp.bfloat16)

    prob_part = lax.all_gather(probabilities, "dp", axis=0, tiled=True)

    with jax.named_scope("dense_expected"):
        onehot = (
            block_lists[:, :, None] == jnp.arange(n_tb, dtype=jnp.int32)[None, None, :]
        ).astype(jnp.bfloat16)
        spread = jnp.einsum(
            "bsk,bsrt->brkt", onehot, prob_part, preferred_element_type=jnp.float32
        ).astype(jnp.bfloat16)
        embedding_part = jnp.einsum(
            "bv,vd->bd",
            spread.reshape(n_blk * BB, n_tb * TB),
            out_weight,
            preferred_element_type=jnp.float32,
        )
    summed = lax.psum_scatter(embedding_part, "vocab", scatter_dimension=0, tiled=True)
    squares = lax.psum(jnp.sum(summed * summed, axis=1), "dp")
    width = hidden.shape[1] * n_vocab
    expected = summed * lax.rsqrt(squares / width + 1e-06)[:, None]
    return (allowed_logprob[None], expected)


def solution(mesh):
    in_specs = (P("dp", "vocab"), P("vocab", "dp"), P("vocab", None, None), P("vocab", None))
    out_specs = (P("vocab", "dp", None, None, None), P("vocab", "dp"))
    return jax.shard_map(
        per_device, mesh=mesh, in_specs=in_specs, out_specs=out_specs, check_vma=False
    )
```

```python
import jax
import jax.numpy as jnp
from jax import lax
from jax.sharding import PartitionSpec as P

TB = 128
BB = 128
MOST = 16


def exchange_stage(x, remaining, bit, n):
    me = lax.axis_index("vocab")
    axis = remaining.index(bit)
    mine = (me // (1 << bit)) % 2
    keep = lax.dynamic_index_in_dim(x, mine, axis=axis, keepdims=False)
    send = lax.dynamic_index_in_dim(x, 1 - mine, axis=axis, keepdims=False)
    perm = [(s, s ^ (1 << bit)) for s in range(n)]
    got = lax.ppermute(send, "vocab", perm=perm)
    return keep + got, [b for b in remaining if b != bit]


def halving_reduce_scatter(part, n):
    levels = n.bit_length() - 1
    rows, cols = part.shape
    group = rows // n
    remaining = list(range(levels - 1, -1, -1))
    x = part.reshape([2] * levels + [group, cols])
    with jax.named_scope("summed_core_stage"):
        x, remaining = exchange_stage(x, remaining, 0, n)
    half = cols // 2
    first, second = x[..., :half], x[..., half:]
    rest_a, rest_b = list(remaining), list(remaining)
    order_a = sorted(remaining)
    order_b = sorted(remaining, reverse=True)
    for step in range(len(order_a)):
        with jax.named_scope("summed_chip_stage"):
            first, rest_a = exchange_stage(first, rest_a, order_a[step], n)
            second, rest_b = exchange_stage(second, rest_b, order_b[step], n)
    return jnp.concatenate([first, second], axis=-1)


def per_device(hidden, out_weight, token_blocks, counts):
    vocab_here, columns_here = out_weight.shape
    n_tb = vocab_here // TB
    block_lists = token_blocks[0]
    block_counts = counts[0]
    n_blk = block_lists.shape[0]
    own_blocks = hidden.shape[0] // BB
    first_block = lax.axis_index("dp") * own_blocks
    own_counts = lax.dynamic_slice_in_dim(block_counts, first_block, own_blocks, 0)

    n_vocab = lax.psum(1, "vocab")
    n_dp = lax.psum(1, "dp")
    with jax.named_scope("hidden_spread"):
        row_slices = lax.all_to_all(hidden, "vocab", split_axis=0, concat_axis=1, tiled=True)
        plane_rows = lax.all_to_all(row_slices, "dp", split_axis=1, concat_axis=0, tiled=True)
        gathered = lax.all_gather(plane_rows, "vocab", axis=0, tiled=True)
        group = hidden.shape[0] // n_vocab
        beam_columns = (
            gathered.reshape(n_vocab, n_dp, group, columns_here)
            .transpose(1, 0, 2, 3)
            .reshape(n_dp * n_vocab * group, columns_here)
        )

    with jax.named_scope("dense_logits"):
        full = jnp.einsum(
            "bd,vd->bv", beam_columns, out_weight, preferred_element_type=jnp.float32
        )
        full4 = full.reshape(n_blk, BB, n_tb, TB)
        rows = jnp.arange(n_blk, dtype=jnp.int32)[:, None]
        picked = full4[rows, :, block_lists, :]

    logits = lax.psum_scatter(picked, "dp", scatter_dimension=0, tiled=True)

    with jax.named_scope("softmax_stats"):
        live = jnp.arange(MOST, dtype=jnp.int32)[None, :] < own_counts[:, None]
        live_mask = live[:, :, None, None]
        masked = jnp.where(live_mask, logits, -jnp.inf)
        local_max = jnp.max(masked, axis=(1, 3))
        local_total = jnp.sum(jnp.exp(masked - local_max[:, None, :, None]), axis=(1, 3))
        stats = lax.all_gather(jnp.stack([local_max, local_total]), "vocab", axis=0)
        beam_max = jnp.max(stats[:, 0], axis=0)
        beam_total = jnp.sum(stats[:, 1] * jnp.exp(stats[:, 0] - beam_max[None]), axis=0)
        shifted = logits - beam_max[:, None, :, None] - jnp.log(beam_total)[:, None, :, None]
        allowed_logprob = jnp.where(live_mask, shifted, 0.0)
        probabilities = jnp.where(live_mask, jnp.exp(shifted), 0.0).astype(jnp.bfloat16)

    prob_part = lax.all_gather(probabilities, "dp", axis=0, tiled=True)

    with jax.named_scope("dense_expected"):
        onehot = (
            block_lists[:, :, None] == jnp.arange(n_tb, dtype=jnp.int32)[None, None, :]
        ).astype(jnp.bfloat16)
        spread = jnp.einsum(
            "bsk,bsrt->brkt", onehot, prob_part, preferred_element_type=jnp.float32
        ).astype(jnp.bfloat16)
        embedding_part = jnp.einsum(
            "bv,vd->bd",
            spread.reshape(n_blk * BB, n_tb * TB),
            out_weight,
            preferred_element_type=jnp.float32,
        )
    summed = halving_reduce_scatter(embedding_part, n_vocab)
    squares = lax.psum(jnp.sum(summed * summed, axis=1), "dp")
    width = hidden.shape[1] * n_vocab
    expected = summed * lax.rsqrt(squares / width + 1e-06)[:, None]
    return (allowed_logprob[None], expected)


def solution(mesh):
    in_specs = (P("dp", "vocab"), P("vocab", "dp"), P("vocab", None, None), P("vocab", None))
    out_specs = (P("vocab", "dp", None, None, None), P("vocab", "dp"))
    return jax.shard_map(
        per_device, mesh=mesh, in_specs=in_specs, out_specs=out_specs, check_vma=False
    )
```

```python
import jax
import jax.numpy as jnp
from jax import lax
from jax.sharding import PartitionSpec as P

TB = 128
BB = 128
MOST = 16


def exchange_stage(x, remaining, bit, n):
    me = lax.axis_index("vocab")
    axis = remaining.index(bit)
    mine = (me // (1 << bit)) % 2
    keep = lax.dynamic_index_in_dim(x, mine, axis=axis, keepdims=False)
    send = lax.dynamic_index_in_dim(x, 1 - mine, axis=axis, keepdims=False)
    perm = [(s, s ^ (1 << bit)) for s in range(n)]
    got = lax.ppermute(send, "vocab", perm=perm)
    return keep + got, [b for b in remaining if b != bit]


def halving_reduce_scatter(part, n):
    levels = n.bit_length() - 1
    rows, cols = part.shape
    group = rows // n
    remaining = list(range(levels - 1, -1, -1))
    x = part.reshape([2] * levels + [group, cols])
    with jax.named_scope("summed_core_stage"):
        x, remaining = exchange_stage(x, remaining, 0, n)
    half = cols // 2
    first, second = x[..., :half], x[..., half:]
    rest_a, rest_b = list(remaining), list(remaining)
    order_a = sorted(remaining)
    order_b = sorted(remaining, reverse=True)
    for step in range(len(order_a)):
        with jax.named_scope("summed_chip_stage"):
            first, rest_a = exchange_stage(first, rest_a, order_a[step], n)
            second, rest_b = exchange_stage(second, rest_b, order_b[step], n)
    return jnp.concatenate([first, second], axis=-1)


def permute_all_to_all(x, axis_name, n, split_axis, concat_axis):
    me = lax.axis_index(axis_name)
    pieces = jnp.stack(jnp.split(x, n, axis=split_axis))
    got = [lax.dynamic_index_in_dim(pieces, me, axis=0, keepdims=False)]
    for shift in range(1, n):
        send = lax.dynamic_index_in_dim(pieces, (me + shift) % n, axis=0, keepdims=False)
        perm = [(s, (s + shift) % n) for s in range(n)]
        got.append(lax.ppermute(send, axis_name, perm=perm))
    received = jnp.stack(got)
    order = (me - jnp.arange(n, dtype=jnp.int32)) % n
    by_source = jnp.take(received, order, axis=0)
    return jnp.concatenate([by_source[k] for k in range(n)], axis=concat_axis)


def gather_stage(x, have, bit, n):
    me = lax.axis_index("vocab")
    mine = (me // (1 << bit)) % 2
    perm = [(s, s ^ (1 << bit)) for s in range(n)]
    got = lax.ppermute(x, "vocab", perm=perm)
    pos = len([b for b in have if b > bit])
    low = jnp.stack([x, got], axis=pos)
    high = jnp.stack([got, x], axis=pos)
    return jnp.where(mine == 0, low, high), sorted(have + [bit], reverse=True)


def doubling_all_gather(x, n):
    levels = n.bit_length() - 1
    rows, cols = x.shape
    half = cols // 2
    first, second = x[:, :half], x[:, half:]
    have_a, have_b = [], []
    order_a = list(range(1, levels)) + [0]
    order_b = list(range(levels - 1, 0, -1)) + [0]
    for step in range(levels):
        with jax.named_scope("hidden_gather_stage"):
            first, have_a = gather_stage(first, have_a, order_a[step], n)
            second, have_b = gather_stage(second, have_b, order_b[step], n)
    joined = jnp.concatenate([first, second], axis=-1)
    return joined.reshape(n * rows, cols)


def per_device(hidden, out_weight, token_blocks, counts):
    vocab_here, columns_here = out_weight.shape
    n_tb = vocab_here // TB
    block_lists = token_blocks[0]
    block_counts = counts[0]
    n_blk = block_lists.shape[0]
    own_blocks = hidden.shape[0] // BB
    first_block = lax.axis_index("dp") * own_blocks
    own_counts = lax.dynamic_slice_in_dim(block_counts, first_block, own_blocks, 0)

    n_vocab = lax.psum(1, "vocab")
    n_dp = lax.psum(1, "dp")
    with jax.named_scope("hidden_spread"):
        row_slices = permute_all_to_all(hidden, "vocab", n_vocab, split_axis=0, concat_axis=1)
        plane_rows = permute_all_to_all(row_slices, "dp", n_dp, split_axis=1, concat_axis=0)
        gathered = doubling_all_gather(plane_rows, n_vocab)
        group = hidden.shape[0] // n_vocab
        beam_columns = (
            gathered.reshape(n_vocab, n_dp, group, columns_here)
            .transpose(1, 0, 2, 3)
            .reshape(n_dp * n_vocab * group, columns_here)
        )

    with jax.named_scope("dense_logits"):
        full = jnp.einsum(
            "bd,vd->bv", beam_columns, out_weight, preferred_element_type=jnp.float32
        )
        full4 = full.reshape(n_blk, BB, n_tb, TB)
        rows = jnp.arange(n_blk, dtype=jnp.int32)[:, None]
        picked = full4[rows, :, block_lists, :]

    logits = lax.psum_scatter(picked, "dp", scatter_dimension=0, tiled=True)

    with jax.named_scope("softmax_stats"):
        live = jnp.arange(MOST, dtype=jnp.int32)[None, :] < own_counts[:, None]
        live_mask = live[:, :, None, None]
        masked = jnp.where(live_mask, logits, -jnp.inf)
        local_max = jnp.max(masked, axis=(1, 3))
        local_total = jnp.sum(jnp.exp(masked - local_max[:, None, :, None]), axis=(1, 3))
        stats = lax.all_gather(jnp.stack([local_max, local_total]), "vocab", axis=0)
        beam_max = jnp.max(stats[:, 0], axis=0)
        beam_total = jnp.sum(stats[:, 1] * jnp.exp(stats[:, 0] - beam_max[None]), axis=0)
        shifted = logits - beam_max[:, None, :, None] - jnp.log(beam_total)[:, None, :, None]
        allowed_logprob = jnp.where(live_mask, shifted, 0.0)
        probabilities = jnp.where(live_mask, jnp.exp(shifted), 0.0).astype(jnp.bfloat16)

    prob_part = lax.all_gather(probabilities, "dp", axis=0, tiled=True)

    with jax.named_scope("dense_expected"):
        onehot = (
            block_lists[:, :, None] == jnp.arange(n_tb, dtype=jnp.int32)[None, None, :]
        ).astype(jnp.bfloat16)
        spread = jnp.einsum(
            "bsk,bsrt->brkt", onehot, prob_part, preferred_element_type=jnp.float32
        ).astype(jnp.bfloat16)
        embedding_part = jnp.einsum(
            "bv,vd->bd",
            spread.reshape(n_blk * BB, n_tb * TB),
            out_weight,
            preferred_element_type=jnp.float32,
        )
    summed = halving_reduce_scatter(embedding_part, n_vocab)
    squares = lax.psum(jnp.sum(summed * summed, axis=1), "dp")
    width = hidden.shape[1] * n_vocab
    expected = summed * lax.rsqrt(squares / width + 1e-06)[:, None]
    return (allowed_logprob[None], expected)


def solution(mesh):
    in_specs = (P("dp", "vocab"), P("vocab", "dp"), P("vocab", None, None), P("vocab", None))
    out_specs = (P("vocab", "dp", None, None, None), P("vocab", "dp"))
    return jax.shard_map(
        per_device, mesh=mesh, in_specs=in_specs, out_specs=out_specs, check_vma=False
    )
```

```python
import jax
import jax.numpy as jnp
from jax import lax
from jax.sharding import PartitionSpec as P

TB = 128
BB = 128
MOST = 16


def exchange_stage(x, remaining, bit, n):
    me = lax.axis_index("vocab")
    axis = remaining.index(bit)
    mine = (me // (1 << bit)) % 2
    keep = lax.dynamic_index_in_dim(x, mine, axis=axis, keepdims=False)
    send = lax.dynamic_index_in_dim(x, 1 - mine, axis=axis, keepdims=False)
    perm = [(s, s ^ (1 << bit)) for s in range(n)]
    got = lax.ppermute(send, "vocab", perm=perm)
    return keep + got, [b for b in remaining if b != bit]


def halving_reduce_scatter(part, n):
    levels = n.bit_length() - 1
    rows, cols = part.shape
    group = rows // n
    remaining = list(range(levels - 1, -1, -1))
    x = part.reshape([2] * levels + [group, cols])
    with jax.named_scope("summed_core_stage"):
        x, remaining = exchange_stage(x, remaining, 0, n)
    half = cols // 2
    first, second = x[..., :half], x[..., half:]
    rest_a, rest_b = list(remaining), list(remaining)
    order_a = sorted(remaining)
    order_b = sorted(remaining, reverse=True)
    for step in range(len(order_a)):
        with jax.named_scope("summed_chip_stage"):
            first, rest_a = exchange_stage(first, rest_a, order_a[step], n)
            second, rest_b = exchange_stage(second, rest_b, order_b[step], n)
    return jnp.concatenate([first, second], axis=-1)


def permute_all_to_all(x, axis_name, n, split_axis, concat_axis):
    me = lax.axis_index(axis_name)
    shape = list(x.shape)
    shape[split_axis : split_axis + 1] = [n, x.shape[split_axis] // n]
    pieces = jnp.moveaxis(x.reshape(shape), split_axis, 0)
    got = [lax.dynamic_index_in_dim(pieces, me, axis=0, keepdims=False)]
    for shift in range(1, n):
        send = lax.dynamic_index_in_dim(pieces, (me + shift) % n, axis=0, keepdims=False)
        perm = [(s, (s + shift) % n) for s in range(n)]
        got.append(lax.ppermute(send, axis_name, perm=perm))
    received = jnp.stack(got)
    order = (me - jnp.arange(n, dtype=jnp.int32)) % n
    by_source = jnp.take(received, order, axis=0)
    return jnp.concatenate([by_source[k] for k in range(n)], axis=concat_axis)


def gather_stage(x, have, bit, n):
    me = lax.axis_index("vocab")
    mine = (me // (1 << bit)) % 2
    perm = [(s, s ^ (1 << bit)) for s in range(n)]
    got = lax.ppermute(x, "vocab", perm=perm)
    pos = len([b for b in have if b > bit])
    low = jnp.stack([x, got], axis=pos)
    high = jnp.stack([got, x], axis=pos)
    return jnp.where(mine == 0, low, high), sorted(have + [bit], reverse=True)


def doubling_all_gather(x, n):
    levels = n.bit_length() - 1
    rows, cols = x.shape
    half = cols // 2
    first, second = x[:, :half], x[:, half:]
    have_a, have_b = [], []
    order_a = list(range(1, levels)) + [0]
    order_b = list(range(levels - 1, 0, -1)) + [0]
    for step in range(levels):
        with jax.named_scope("hidden_gather_stage"):
            first, have_a = gather_stage(first, have_a, order_a[step], n)
            second, have_b = gather_stage(second, have_b, order_b[step], n)
    joined = jnp.concatenate([first, second], axis=-1)
    return joined.reshape(n * rows, cols)


def small_all_gather(x, n):
    levels = n.bit_length() - 1
    have = []
    y = x
    for bit in range(levels):
        y, have = gather_stage(y, have, bit, n)
    return y.reshape((n,) + x.shape)


def butterfly_sum(x, axis_name, n):
    levels = n.bit_length() - 1
    for bit in range(levels):
        perm = [(s, s ^ (1 << bit)) for s in range(n)]
        x = x + lax.ppermute(x, axis_name, perm=perm)
    return x


def spread_block(probs_block, tokens, n_tb):
    onehot = (tokens[:, None] == jnp.arange(n_tb, dtype=jnp.int32)[None, :]).astype(
        jnp.bfloat16
    )
    spread = jnp.einsum(
        "sk,srt->rkt", onehot, probs_block, preferred_element_type=jnp.float32
    ).astype(jnp.bfloat16)
    return spread.reshape(spread.shape[0], -1)


def ring_expected(own_probs, block_lists, out_weight, n, n_blk, n_tb):
    me = lax.axis_index("dp")
    columns = out_weight.shape[1]
    rows_per = own_probs.shape[1]
    acc = jnp.zeros((n_blk, rows_per, columns), jnp.float32)

    def add_piece(acc, piece, block):
        block = jnp.clip(block, 0, n - 1)
        tokens = lax.dynamic_index_in_dim(block_lists, block, axis=0, keepdims=False)
        term = jnp.dot(
            spread_block(piece, tokens, n_tb), out_weight, preferred_element_type=jnp.float32
        )
        old = lax.dynamic_index_in_dim(acc, block, axis=0, keepdims=False)
        return lax.dynamic_update_index_in_dim(acc, old + term, block, axis=0)

    acc = add_piece(acc, own_probs, me)
    from_left, from_right = own_probs, own_probs
    for step in range(1, n):
        rightward = [(s, s + 1) for s in range(step - 1, n - 1)]
        leftward = [(s, s - 1) for s in range(1, n - step + 1)]
        from_left = lax.ppermute(from_left, "dp", perm=rightward)
        from_right = lax.ppermute(from_right, "dp", perm=leftward)
        acc = add_piece(acc, from_left, me - step)
        acc = add_piece(acc, from_right, me + step)
    return acc.reshape(n_blk * rows_per, columns)


def per_device(hidden, out_weight, token_blocks, counts):
    vocab_here, columns_here = out_weight.shape
    n_tb = vocab_here // TB
    block_lists = token_blocks[0]
    block_counts = counts[0]
    n_blk = block_lists.shape[0]
    own_blocks = hidden.shape[0] // BB
    first_block = lax.axis_index("dp") * own_blocks
    own_counts = lax.dynamic_slice_in_dim(block_counts, first_block, own_blocks, 0)
    assert own_blocks == 1 and n_blk == lax.psum(1, "dp")

    n_vocab = lax.psum(1, "vocab")
    n_dp = lax.psum(1, "dp")
    with jax.named_scope("hidden_spread"):
        row_slices = permute_all_to_all(hidden, "vocab", n_vocab, split_axis=0, concat_axis=1)
        plane_rows = permute_all_to_all(row_slices, "dp", n_dp, split_axis=1, concat_axis=0)
        gathered = doubling_all_gather(plane_rows, n_vocab)
        group = hidden.shape[0] // n_vocab
        beam_columns = (
            gathered.reshape(n_vocab, n_dp, group, columns_here)
            .transpose(1, 0, 2, 3)
            .reshape(n_dp * n_vocab * group, columns_here)
        )

    with jax.named_scope("dense_logits"):
        full = jnp.einsum(
            "bd,vd->bv", beam_columns, out_weight, preferred_element_type=jnp.float32
        )
        full4 = full.reshape(n_blk, BB, n_tb, TB)
        rows = jnp.arange(n_blk, dtype=jnp.int32)[:, None]
        picked = full4[rows, :, block_lists, :]

    logits = lax.psum_scatter(picked, "dp", scatter_dimension=0, tiled=True)

    with jax.named_scope("softmax_stats"):
        live = jnp.arange(MOST, dtype=jnp.int32)[None, :] < own_counts[:, None]
        live_mask = live[:, :, None, None]
        masked = jnp.where(live_mask, logits, -jnp.inf)
        local_max = jnp.max(masked, axis=(1, 3))
        local_total = jnp.sum(jnp.exp(masked - local_max[:, None, :, None]), axis=(1, 3))
        stats = small_all_gather(jnp.stack([local_max, local_total]), n_vocab)
        beam_max = jnp.max(stats[:, 0], axis=0)
        beam_total = jnp.sum(stats[:, 1] * jnp.exp(stats[:, 0] - beam_max[None]), axis=0)
        shifted = logits - beam_max[:, None, :, None] - jnp.log(beam_total)[:, None, :, None]
        allowed_logprob = jnp.where(live_mask, shifted, 0.0)
        probabilities = jnp.where(live_mask, jnp.exp(shifted), 0.0).astype(jnp.bfloat16)

    with jax.named_scope("expected_ring"):
        embedding_part = ring_expected(
            probabilities[0], block_lists, out_weight, n_dp, n_blk, n_tb
        )
    summed = halving_reduce_scatter(embedding_part, n_vocab)
    squares = butterfly_sum(jnp.sum(summed * summed, axis=1), "dp", n_dp)
    width = hidden.shape[1] * n_vocab
    expected = summed * lax.rsqrt(squares / width + 1e-06)[:, None]
    return (allowed_logprob[None], expected)


def solution(mesh):
    in_specs = (P("dp", "vocab"), P("vocab", "dp"), P("vocab", None, None), P("vocab", None))
    out_specs = (P("vocab", "dp", None, None, None), P("vocab", "dp"))
    return jax.shard_map(
        per_device, mesh=mesh, in_specs=in_specs, out_specs=out_specs, check_vma=False
    )
```

```python
import jax
import jax.numpy as jnp
from jax import lax
from jax.sharding import PartitionSpec as P

TB = 128
BB = 128
MOST = 16


def exchange_stage(x, remaining, bit, n):
    me = lax.axis_index("vocab")
    axis = remaining.index(bit)
    mine = (me // (1 << bit)) % 2
    keep = lax.dynamic_index_in_dim(x, mine, axis=axis, keepdims=False)
    send = lax.dynamic_index_in_dim(x, 1 - mine, axis=axis, keepdims=False)
    perm = [(s, s ^ (1 << bit)) for s in range(n)]
    got = lax.ppermute(send, "vocab", perm=perm)
    return keep + got, [b for b in remaining if b != bit]


def halving_reduce_scatter(part, n):
    levels = n.bit_length() - 1
    rows, cols = part.shape
    group = rows // n
    remaining = list(range(levels - 1, -1, -1))
    x = part.reshape([2] * levels + [group, cols])
    with jax.named_scope("summed_core_stage"):
        x, remaining = exchange_stage(x, remaining, 0, n)
    half = cols // 2
    first, second = x[..., :half], x[..., half:]
    rest_a, rest_b = list(remaining), list(remaining)
    order_a = sorted(remaining)
    order_b = sorted(remaining, reverse=True)
    for step in range(len(order_a)):
        with jax.named_scope("summed_chip_stage"):
            first, rest_a = exchange_stage(first, rest_a, order_a[step], n)
            second, rest_b = exchange_stage(second, rest_b, order_b[step], n)
    return jnp.concatenate([first, second], axis=-1)


def permute_all_to_all(x, axis_name, n, split_axis, concat_axis):
    me = lax.axis_index(axis_name)
    shape = list(x.shape)
    shape[split_axis : split_axis + 1] = [n, x.shape[split_axis] // n]
    pieces = jnp.moveaxis(x.reshape(shape), split_axis, 0)
    got = [lax.dynamic_index_in_dim(pieces, me, axis=0, keepdims=False)]
    for shift in range(1, n):
        send = lax.dynamic_index_in_dim(pieces, (me + shift) % n, axis=0, keepdims=False)
        perm = [(s, (s + shift) % n) for s in range(n)]
        got.append(lax.ppermute(send, axis_name, perm=perm))
    received = jnp.stack(got)
    order = (me - jnp.arange(n, dtype=jnp.int32)) % n
    by_source = jnp.take(received, order, axis=0)
    return jnp.concatenate([by_source[k] for k in range(n)], axis=concat_axis)


def gather_stage(x, have, bit, n):
    me = lax.axis_index("vocab")
    mine = (me // (1 << bit)) % 2
    perm = [(s, s ^ (1 << bit)) for s in range(n)]
    got = lax.ppermute(x, "vocab", perm=perm)
    pos = len([b for b in have if b > bit])
    low = jnp.stack([x, got], axis=pos)
    high = jnp.stack([got, x], axis=pos)
    return jnp.where(mine == 0, low, high), sorted(have + [bit], reverse=True)


def doubling_all_gather(x, n):
    levels = n.bit_length() - 1
    rows, cols = x.shape
    half = cols // 2
    first, second = x[:, :half], x[:, half:]
    have_a, have_b = [], []
    order_a = list(range(1, levels)) + [0]
    order_b = list(range(levels - 1, 0, -1)) + [0]
    for step in range(levels):
        with jax.named_scope("hidden_gather_stage"):
            first, have_a = gather_stage(first, have_a, order_a[step], n)
            second, have_b = gather_stage(second, have_b, order_b[step], n)
    joined = jnp.concatenate([first, second], axis=-1)
    return joined.reshape(n * rows, cols)


def small_all_gather(x, n):
    levels = n.bit_length() - 1
    have = []
    y = x
    for bit in range(levels):
        y, have = gather_stage(y, have, bit, n)
    return y.reshape((n,) + x.shape)


def butterfly_sum(x, axis_name, n):
    levels = n.bit_length() - 1
    for bit in range(levels):
        perm = [(s, s ^ (1 << bit)) for s in range(n)]
        x = x + lax.ppermute(x, axis_name, perm=perm)
    return x


def spread_block(probs_block, tokens, n_tb):
    onehot = (tokens[:, None] == jnp.arange(n_tb, dtype=jnp.int32)[None, :]).astype(
        jnp.bfloat16
    )
    spread = jnp.einsum(
        "sk,srt->rkt", onehot, probs_block, preferred_element_type=jnp.float32
    ).astype(jnp.bfloat16)
    return spread.reshape(spread.shape[0], -1)


def ring_expected(own_probs, block_lists, out_weight, n, n_blk, n_tb):
    me = lax.axis_index("dp")
    columns = out_weight.shape[1]
    rows_per = own_probs.shape[1]
    acc = jnp.zeros((n_blk, rows_per, columns), jnp.float32)

    def add_piece(acc, piece, block):
        block = jnp.clip(block, 0, n - 1)
        tokens = lax.dynamic_index_in_dim(block_lists, block, axis=0, keepdims=False)
        term = jnp.dot(
            spread_block(piece, tokens, n_tb), out_weight, preferred_element_type=jnp.float32
        )
        old = lax.dynamic_index_in_dim(acc, block, axis=0, keepdims=False)
        return lax.dynamic_update_index_in_dim(acc, old + term, block, axis=0)

    acc = add_piece(acc, own_probs, me)
    from_left, from_right = own_probs, own_probs
    for step in range(1, n):
        rightward = [(s, s + 1) for s in range(step - 1, n - 1)]
        leftward = [(s, s - 1) for s in range(1, n - step + 1)]
        from_left = lax.ppermute(from_left, "dp", perm=rightward)
        from_right = lax.ppermute(from_right, "dp", perm=leftward)
        acc = add_piece(acc, from_left, me - step)
        acc = add_piece(acc, from_right, me + step)
    return acc.reshape(n_blk * rows_per, columns)


def per_device(hidden, out_weight, token_blocks, counts):
    vocab_here, columns_here = out_weight.shape
    n_vocab = lax.psum(1, "vocab")
    n_dp = lax.psum(1, "dp")
    n_tb = vocab_here // TB
    block_lists = token_blocks[0]
    block_counts = counts[0]
    n_blk = block_lists.shape[0]
    own_blocks = hidden.shape[0] // BB
    assert own_blocks == 1 and n_blk == n_dp
    me_dp = lax.axis_index("dp")
    own_counts = lax.dynamic_slice_in_dim(block_counts, me_dp, 1, 0)
    rows_per_dev = n_blk * BB // n_vocab
    devs_per_block = BB // rows_per_dev
    half_rows = rows_per_dev // 2

    with jax.named_scope("hidden_spread"):
        row_slices = permute_all_to_all(hidden, "vocab", n_vocab, split_axis=0, concat_axis=1)
        plane_rows = permute_all_to_all(row_slices, "dp", n_dp, split_axis=1, concat_axis=0)
        gathered = doubling_all_gather(plane_rows, n_vocab)
        group = hidden.shape[0] // n_vocab
        beam_columns = (
            gathered.reshape(n_vocab, n_dp, group, columns_here)
            .transpose(1, 0, 2, 3)
            .reshape(n_blk, devs_per_block, 2, half_rows, columns_here)
        )

    live = jnp.arange(MOST, dtype=jnp.int32)[None, :] < own_counts[:, None]
    live_mask = live[:, :, None, None]
    block_ids = jnp.arange(n_blk, dtype=jnp.int32)[:, None]
    onehot = (
        block_lists[:, :, None] == jnp.arange(n_tb, dtype=jnp.int32)[None, None, :]
    ).astype(jnp.bfloat16)

    logprob_parts, summed_parts = [], []
    for part in range(2):
        with jax.named_scope("dense_logits"):
            beams = beam_columns[:, :, part].reshape(n_blk * BB // 2, columns_here)
            full = jnp.einsum(
                "bd,vd->bv", beams, out_weight, preferred_element_type=jnp.float32
            )
            full4 = full.reshape(n_blk, BB // 2, n_tb, TB)
            picked = full4[block_ids, :, block_lists, :]
        logits = lax.psum_scatter(picked, "dp", scatter_dimension=0, tiled=True)

        with jax.named_scope("softmax_stats"):
            masked = jnp.where(live_mask, logits, -jnp.inf)
            local_max = jnp.max(masked, axis=(1, 3))
            local_total = jnp.sum(jnp.exp(masked - local_max[:, None, :, None]), axis=(1, 3))
            stats = lax.all_gather(jnp.stack([local_max, local_total]), "vocab", axis=0)
            beam_max = jnp.max(stats[:, 0], axis=0)
            beam_total = jnp.sum(stats[:, 1] * jnp.exp(stats[:, 0] - beam_max[None]), axis=0)
            shifted = logits - beam_max[:, None, :, None] - jnp.log(beam_total)[:, None, :, None]
            logprob_parts.append(jnp.where(live_mask, shifted, 0.0))
            probabilities = jnp.where(live_mask, jnp.exp(shifted), 0.0).astype(jnp.bfloat16)

        prob_part = lax.all_gather(probabilities, "dp", axis=0, tiled=True)

        with jax.named_scope("dense_expected"):
            spread = jnp.einsum(
                "bsk,bsrt->brkt", onehot, prob_part, preferred_element_type=jnp.float32
            ).astype(jnp.bfloat16)
            embedding_part = jnp.einsum(
                "bv,vd->bd",
                spread.reshape(n_blk * BB // 2, n_tb * TB),
                out_weight,
                preferred_element_type=jnp.float32,
            )
        summed_parts.append(halving_reduce_scatter(embedding_part, n_vocab))

    def interleave(a, b, axis):
        shape = a.shape[:axis] + (devs_per_block, half_rows) + a.shape[axis + 1 :]
        joined = jnp.stack([a.reshape(shape), b.reshape(shape)], axis=axis + 1)
        return joined.reshape(a.shape[:axis] + (2 * a.shape[axis],) + a.shape[axis + 1 :])

    allowed_logprob = interleave(logprob_parts[0], logprob_parts[1], 2)
    summed = jnp.concatenate(summed_parts, axis=0)
    squares = butterfly_sum(jnp.sum(summed * summed, axis=1), "dp", n_dp)
    width = hidden.shape[1] * n_vocab
    expected = summed * lax.rsqrt(squares / width + 1e-06)[:, None]
    return (allowed_logprob[None], expected)


def solution(mesh):
    in_specs = (P("dp", "vocab"), P("vocab", "dp"), P("vocab", None, None), P("vocab", None))
    out_specs = (P("vocab", "dp", None, None, None), P("vocab", "dp"))
    return jax.shard_map(
        per_device, mesh=mesh, in_specs=in_specs, out_specs=out_specs, check_vma=False
    )
```

```python
import jax
import jax.numpy as jnp
from jax import lax
from jax.sharding import PartitionSpec as P

TB = 128
BB = 128
MOST = 16


def exchange_stage(x, remaining, bit, n):
    me = lax.axis_index("vocab")
    axis = remaining.index(bit)
    mine = (me // (1 << bit)) % 2
    keep = lax.dynamic_index_in_dim(x, mine, axis=axis, keepdims=False)
    send = lax.dynamic_index_in_dim(x, 1 - mine, axis=axis, keepdims=False)
    perm = [(s, s ^ (1 << bit)) for s in range(n)]
    got = lax.ppermute(send, "vocab", perm=perm)
    return keep + got, [b for b in remaining if b != bit]


def halving_reduce_scatter(part, n):
    levels = n.bit_length() - 1
    rows, cols = part.shape
    group = rows // n
    remaining = list(range(levels - 1, -1, -1))
    x = part.reshape([2] * levels + [group, cols])
    with jax.named_scope("summed_core_stage"):
        x, remaining = exchange_stage(x, remaining, 0, n)
    half = cols // 2
    first, second = x[..., :half], x[..., half:]
    rest_a, rest_b = list(remaining), list(remaining)
    order_a = sorted(remaining)
    order_b = sorted(remaining, reverse=True)
    for step in range(len(order_a)):
        with jax.named_scope("summed_chip_stage"):
            first, rest_a = exchange_stage(first, rest_a, order_a[step], n)
            second, rest_b = exchange_stage(second, rest_b, order_b[step], n)
    return jnp.concatenate([first, second], axis=-1)


def permute_all_to_all(x, axis_name, n, split_axis, concat_axis):
    me = lax.axis_index(axis_name)
    shape = list(x.shape)
    shape[split_axis : split_axis + 1] = [n, x.shape[split_axis] // n]
    pieces = jnp.moveaxis(x.reshape(shape), split_axis, 0)
    got = [lax.dynamic_index_in_dim(pieces, me, axis=0, keepdims=False)]
    for shift in range(1, n):
        send = lax.dynamic_index_in_dim(pieces, (me + shift) % n, axis=0, keepdims=False)
        perm = [(s, (s + shift) % n) for s in range(n)]
        got.append(lax.ppermute(send, axis_name, perm=perm))
    received = jnp.stack(got)
    order = (me - jnp.arange(n, dtype=jnp.int32)) % n
    by_source = jnp.take(received, order, axis=0)
    return jnp.concatenate([by_source[k] for k in range(n)], axis=concat_axis)


def gather_stage(x, have, bit, n):
    me = lax.axis_index("vocab")
    mine = (me // (1 << bit)) % 2
    perm = [(s, s ^ (1 << bit)) for s in range(n)]
    got = lax.ppermute(x, "vocab", perm=perm)
    pos = len([b for b in have if b > bit])
    low = jnp.stack([x, got], axis=pos)
    high = jnp.stack([got, x], axis=pos)
    return jnp.where(mine == 0, low, high), sorted(have + [bit], reverse=True)


def doubling_all_gather(x, n):
    levels = n.bit_length() - 1
    rows, cols = x.shape
    half = cols // 2
    first, second = x[:, :half], x[:, half:]
    have_a, have_b = [], []
    order_a = list(range(1, levels)) + [0]
    order_b = list(range(levels - 1, 0, -1)) + [0]
    for step in range(levels):
        with jax.named_scope("hidden_gather_stage"):
            first, have_a = gather_stage(first, have_a, order_a[step], n)
            second, have_b = gather_stage(second, have_b, order_b[step], n)
    joined = jnp.concatenate([first, second], axis=-1)
    return joined.reshape(n * rows, cols)


def small_all_gather(x, n):
    levels = n.bit_length() - 1
    have = []
    y = x
    for bit in range(levels):
        y, have = gather_stage(y, have, bit, n)
    return y.reshape((n,) + x.shape)


def butterfly_sum(x, axis_name, n):
    levels = n.bit_length() - 1
    for bit in range(levels):
        perm = [(s, s ^ (1 << bit)) for s in range(n)]
        x = x + lax.ppermute(x, axis_name, perm=perm)
    return x


def line_reduce_scatter(partials, n):
    me = lax.axis_index("dp")
    own = lambda block: lax.dynamic_index_in_dim(
        partials, jnp.clip(block, 0, n - 1), axis=0, keepdims=False
    )
    from_left = None
    from_right = None
    for step in range(1, n):
        send_up = own(me + n - step)
        if from_left is not None:
            send_up = send_up + from_left
        send_down = own(me - n + step)
        if from_right is not None:
            send_down = send_down + from_right
        upward = [(s, s + 1) for s in range(0, step)]
        downward = [(s, s - 1) for s in range(n - step, n)]
        from_left = lax.ppermute(send_up, "dp", perm=upward)
        from_right = lax.ppermute(send_down, "dp", perm=downward)
    return (own(me) + from_left + from_right)[None]


def per_device(hidden, out_weight, token_blocks, counts):
    vocab_here, columns_here = out_weight.shape
    n_vocab = lax.psum(1, "vocab")
    n_dp = lax.psum(1, "dp")
    n_tb = vocab_here // TB
    block_lists = token_blocks[0]
    block_counts = counts[0]
    n_blk = block_lists.shape[0]
    own_blocks = hidden.shape[0] // BB
    assert own_blocks == 1 and n_blk == n_dp
    me_dp = lax.axis_index("dp")
    own_counts = lax.dynamic_slice_in_dim(block_counts, me_dp, 1, 0)

    with jax.named_scope("hidden_spread"):
        row_slices = permute_all_to_all(hidden, "vocab", n_vocab, split_axis=0, concat_axis=1)
        plane_rows = permute_all_to_all(row_slices, "dp", n_dp, split_axis=1, concat_axis=0)
        gathered = doubling_all_gather(plane_rows, n_vocab)
        group = hidden.shape[0] // n_vocab
        beam_columns = (
            gathered.reshape(n_vocab, n_dp, group, columns_here)
            .transpose(1, 0, 2, 3)
            .reshape(n_dp * n_vocab * group, columns_here)
        )

    with jax.named_scope("dense_logits"):
        full = jnp.einsum(
            "bd,vd->bv", beam_columns, out_weight, preferred_element_type=jnp.float32
        )
        full4 = full.reshape(n_blk, BB, n_tb, TB)
        rows = jnp.arange(n_blk, dtype=jnp.int32)[:, None]
        picked = full4[rows, :, block_lists, :]

    with jax.named_scope("logits_line_reduce"):
        logits = line_reduce_scatter(picked, n_dp)

    with jax.named_scope("softmax_stats"):
        live = jnp.arange(MOST, dtype=jnp.int32)[None, :] < own_counts[:, None]
        live_mask = live[:, :, None, None]
        masked = jnp.where(live_mask, logits, -jnp.inf)
        local_max = jnp.max(masked, axis=(1, 3))
        local_total = jnp.sum(jnp.exp(masked - local_max[:, None, :, None]), axis=(1, 3))
        stats = lax.all_gather(jnp.stack([local_max, local_total]), "vocab", axis=0)
        beam_max = jnp.max(stats[:, 0], axis=0)
        beam_total = jnp.sum(stats[:, 1] * jnp.exp(stats[:, 0] - beam_max[None]), axis=0)
        shifted = logits - beam_max[:, None, :, None] - jnp.log(beam_total)[:, None, :, None]
        allowed_logprob = jnp.where(live_mask, shifted, 0.0)
        probabilities = jnp.where(live_mask, jnp.exp(shifted), 0.0).astype(jnp.bfloat16)

    prob_part = lax.all_gather(probabilities, "dp", axis=0, tiled=True)

    with jax.named_scope("dense_expected"):
        onehot = (
            block_lists[:, :, None] == jnp.arange(n_tb, dtype=jnp.int32)[None, None, :]
        ).astype(jnp.bfloat16)
        spread = jnp.einsum(
            "bsk,bsrt->brkt", onehot, prob_part, preferred_element_type=jnp.float32
        ).astype(jnp.bfloat16)
        embedding_part = jnp.einsum(
            "bv,vd->bd",
            spread.reshape(n_blk * BB, n_tb * TB),
            out_weight,
            preferred_element_type=jnp.float32,
        )
    summed = halving_reduce_scatter(embedding_part, n_vocab)
    squares = butterfly_sum(jnp.sum(summed * summed, axis=1), "dp", n_dp)
    width = hidden.shape[1] * n_vocab
    expected = summed * lax.rsqrt(squares / width + 1e-06)[:, None]
    return (allowed_logprob[None], expected)


def solution(mesh):
    in_specs = (P("dp", "vocab"), P("vocab", "dp"), P("vocab", None, None), P("vocab", None))
    out_specs = (P("vocab", "dp", None, None, None), P("vocab", "dp"))
    return jax.shard_map(
        per_device, mesh=mesh, in_specs=in_specs, out_specs=out_specs, check_vma=False
    )
```

```python
import jax
import jax.numpy as jnp
from jax import lax
from jax.sharding import PartitionSpec as P

TB = 128
BB = 128
MOST = 16


def exchange_stage(x, remaining, bit, n):
    me = lax.axis_index("vocab")
    axis = remaining.index(bit)
    mine = (me // (1 << bit)) % 2
    keep = lax.dynamic_index_in_dim(x, mine, axis=axis, keepdims=False)
    send = lax.dynamic_index_in_dim(x, 1 - mine, axis=axis, keepdims=False)
    perm = [(s, s ^ (1 << bit)) for s in range(n)]
    got = lax.ppermute(send, "vocab", perm=perm)
    return keep + got, [b for b in remaining if b != bit]


def halving_reduce_scatter(part, n):
    levels = n.bit_length() - 1
    rows, cols = part.shape
    group = rows // n
    remaining = list(range(levels - 1, -1, -1))
    x = part.reshape([2] * levels + [group, cols])
    with jax.named_scope("summed_core_stage"):
        x, remaining = exchange_stage(x, remaining, 0, n)
    half = cols // 2
    first, second = x[..., :half], x[..., half:]
    rest_a, rest_b = list(remaining), list(remaining)
    order_a = sorted(remaining)
    order_b = sorted(remaining, reverse=True)
    for step in range(len(order_a)):
        with jax.named_scope("summed_chip_stage"):
            first, rest_a = exchange_stage(first, rest_a, order_a[step], n)
            second, rest_b = exchange_stage(second, rest_b, order_b[step], n)
    return jnp.concatenate([first, second], axis=-1)


def permute_all_to_all(x, axis_name, n, split_axis, concat_axis):
    me = lax.axis_index(axis_name)
    shape = list(x.shape)
    shape[split_axis : split_axis + 1] = [n, x.shape[split_axis] // n]
    pieces = jnp.moveaxis(x.reshape(shape), split_axis, 0)
    got = [lax.dynamic_index_in_dim(pieces, me, axis=0, keepdims=False)]
    for shift in range(1, n):
        send = lax.dynamic_index_in_dim(pieces, (me + shift) % n, axis=0, keepdims=False)
        perm = [(s, (s + shift) % n) for s in range(n)]
        got.append(lax.ppermute(send, axis_name, perm=perm))
    received = jnp.stack(got)
    order = (me - jnp.arange(n, dtype=jnp.int32)) % n
    by_source = jnp.take(received, order, axis=0)
    return jnp.concatenate([by_source[k] for k in range(n)], axis=concat_axis)


def gather_stage(x, have, bit, n):
    me = lax.axis_index("vocab")
    mine = (me // (1 << bit)) % 2
    perm = [(s, s ^ (1 << bit)) for s in range(n)]
    got = lax.ppermute(x, "vocab", perm=perm)
    pos = len([b for b in have if b > bit])
    low = jnp.stack([x, got], axis=pos)
    high = jnp.stack([got, x], axis=pos)
    return jnp.where(mine == 0, low, high), sorted(have + [bit], reverse=True)


def doubling_all_gather(x, n):
    levels = n.bit_length() - 1
    rows, cols = x.shape
    half = cols // 2
    first, second = x[:, :half], x[:, half:]
    have_a, have_b = [], []
    order_a = list(range(1, levels)) + [0]
    order_b = list(range(levels - 1, 0, -1)) + [0]
    for step in range(levels):
        with jax.named_scope("hidden_gather_stage"):
            first, have_a = gather_stage(first, have_a, order_a[step], n)
            second, have_b = gather_stage(second, have_b, order_b[step], n)
    joined = jnp.concatenate([first, second], axis=-1)
    return joined.reshape(n * rows, cols)


def butterfly_sum(x, axis_name, n):
    levels = n.bit_length() - 1
    for bit in range(levels):
        perm = [(s, s ^ (1 << bit)) for s in range(n)]
        x = x + lax.ppermute(x, axis_name, perm=perm)
    return x


def per_device(hidden, out_weight, token_blocks, counts):
    vocab_here, columns_here = out_weight.shape
    n_vocab = lax.psum(1, "vocab")
    n_dp = lax.psum(1, "dp")
    n_tb = vocab_here // TB
    block_lists = token_blocks[0]
    block_counts = counts[0]
    n_blk = block_lists.shape[0]
    own_blocks = hidden.shape[0] // BB
    assert own_blocks == 1 and n_blk == n_dp
    me_dp = lax.axis_index("dp")
    own_counts = lax.dynamic_slice_in_dim(block_counts, me_dp, 1, 0)

    with jax.named_scope("hidden_spread"):
        row_slices = permute_all_to_all(hidden, "vocab", n_vocab, split_axis=0, concat_axis=1)
        plane_rows = permute_all_to_all(row_slices, "dp", n_dp, split_axis=1, concat_axis=0)
        gathered = doubling_all_gather(plane_rows, n_vocab)
        group = hidden.shape[0] // n_vocab
        beam_columns = (
            gathered.reshape(n_vocab, n_dp, group, columns_here)
            .transpose(1, 0, 2, 3)
            .reshape(n_dp * n_vocab * group, columns_here)
        )

    with jax.named_scope("dense_logits"):
        full = jnp.einsum(
            "bd,vd->bv", beam_columns, out_weight, preferred_element_type=jnp.float32
        )
        full4 = full.reshape(n_blk, BB, n_tb, TB)
        rows = jnp.arange(n_blk, dtype=jnp.int32)[:, None]
        picked = full4[rows, :, block_lists, :]

    logits = lax.psum_scatter(picked, "dp", scatter_dimension=0, tiled=True)

    with jax.named_scope("softmax_stats"):
        live = jnp.arange(MOST, dtype=jnp.int32)[None, :] < own_counts[:, None]
        live_mask = live[:, :, None, None]
        masked = jnp.where(live_mask, logits, -jnp.inf)
        local_max = jnp.max(masked, axis=(1, 3))
        local_total = jnp.sum(jnp.exp(masked - local_max[:, None, :, None]), axis=(1, 3))
        stats = lax.all_gather(jnp.stack([local_max, local_total]), "vocab", axis=0)
        beam_max = jnp.max(stats[:, 0], axis=0)
        beam_total = jnp.sum(stats[:, 1] * jnp.exp(stats[:, 0] - beam_max[None]), axis=0)
        shifted = logits - beam_max[:, None, :, None] - jnp.log(beam_total)[:, None, :, None]
        allowed_logprob = jnp.where(live_mask, shifted, 0.0)
        probabilities = jnp.where(live_mask, jnp.exp(shifted), 0.0).astype(jnp.bfloat16)

    prob_part = lax.all_gather(probabilities, "dp", axis=0, tiled=True)

    with jax.named_scope("dense_expected"):
        onehot = (
            block_lists[:, :, None] == jnp.arange(n_tb, dtype=jnp.int32)[None, None, :]
        ).astype(jnp.bfloat16)
        spread = jnp.einsum(
            "bsk,bsrt->brkt", onehot, prob_part, preferred_element_type=jnp.float32
        ).astype(jnp.bfloat16)
        embedding_part = jnp.einsum(
            "bv,vd->bd",
            spread.reshape(n_blk * BB, n_tb * TB),
            out_weight,
            preferred_element_type=jnp.float32,
        )
    summed = halving_reduce_scatter(embedding_part, n_vocab)
    squares = butterfly_sum(jnp.sum(summed * summed, axis=1), "dp", n_dp)
    width = hidden.shape[1] * n_vocab
    expected = summed * lax.rsqrt(squares / width + 1e-06)[:, None]
    return (allowed_logprob[None], expected)


def solution(mesh):
    in_specs = (P("dp", "vocab"), P("vocab", "dp"), P("vocab", None, None), P("vocab", None))
    out_specs = (P("vocab", "dp", None, None, None), P("vocab", "dp"))
    return jax.shard_map(
        per_device, mesh=mesh, in_specs=in_specs, out_specs=out_specs, check_vma=False
    )
```

```python
import jax
import jax.numpy as jnp
from jax import lax
from jax.sharding import PartitionSpec as P

TB = 128
BB = 128
MOST = 16


def exchange_stage(x, remaining, bit, n):
    me = lax.axis_index("vocab")
    axis = remaining.index(bit)
    mine = (me // (1 << bit)) % 2
    keep = lax.dynamic_index_in_dim(x, mine, axis=axis, keepdims=False)
    send = lax.dynamic_index_in_dim(x, 1 - mine, axis=axis, keepdims=False)
    perm = [(s, s ^ (1 << bit)) for s in range(n)]
    got = lax.ppermute(send, "vocab", perm=perm)
    return keep + got, [b for b in remaining if b != bit]


def halving_reduce_scatter(part, n):
    levels = n.bit_length() - 1
    rows, cols = part.shape
    group = rows // n
    remaining = list(range(levels - 1, -1, -1))
    x = part.reshape([2] * levels + [group, cols])
    with jax.named_scope("summed_core_stage"):
        x, remaining = exchange_stage(x, remaining, 0, n)
    half = cols // 2
    first, second = x[..., :half], x[..., half:]
    rest_a, rest_b = list(remaining), list(remaining)
    order_a = sorted(remaining)
    order_b = sorted(remaining, reverse=True)
    for step in range(len(order_a)):
        with jax.named_scope("summed_chip_stage"):
            first, rest_a = exchange_stage(first, rest_a, order_a[step], n)
            second, rest_b = exchange_stage(second, rest_b, order_b[step], n)
    return jnp.concatenate([first, second], axis=-1)


def gather_stage(x, have, bit, n):
    me = lax.axis_index("vocab")
    mine = (me // (1 << bit)) % 2
    perm = [(s, s ^ (1 << bit)) for s in range(n)]
    got = lax.ppermute(x, "vocab", perm=perm)
    pos = len([b for b in have if b > bit])
    low = jnp.stack([x, got], axis=pos)
    high = jnp.stack([got, x], axis=pos)
    return jnp.where(mine == 0, low, high), sorted(have + [bit], reverse=True)


def doubling_all_gather(x, n):
    levels = n.bit_length() - 1
    rows, cols = x.shape
    half = cols // 2
    first, second = x[:, :half], x[:, half:]
    have_a, have_b = [], []
    order_a = list(range(1, levels)) + [0]
    order_b = list(range(levels - 1, 0, -1)) + [0]
    for step in range(levels):
        with jax.named_scope("hidden_gather_stage"):
            first, have_a = gather_stage(first, have_a, order_a[step], n)
            second, have_b = gather_stage(second, have_b, order_b[step], n)
    joined = jnp.concatenate([first, second], axis=-1)
    return joined.reshape(n * rows, cols)


def butterfly_sum(x, axis_name, n):
    levels = n.bit_length() - 1
    for bit in range(levels):
        perm = [(s, s ^ (1 << bit)) for s in range(n)]
        x = x + lax.ppermute(x, axis_name, perm=perm)
    return x


def bruck_all_to_all(x, axis_name, n, split_axis, concat_axis):
    me = lax.axis_index(axis_name)
    levels = n.bit_length() - 1
    shape = list(x.shape)
    shape[split_axis : split_axis + 1] = [n, x.shape[split_axis] // n]
    pieces = jnp.moveaxis(x.reshape(shape), split_axis, 0)
    rest = pieces.shape[1:]
    held = pieces.reshape([2] * levels + list(rest))
    for bit in range(levels):
        pos = levels - 1 - bit
        mine = (me // (1 << bit)) % 2
        keep = lax.dynamic_index_in_dim(held, mine, axis=pos, keepdims=False)
        send = lax.dynamic_index_in_dim(held, 1 - mine, axis=pos, keepdims=False)
        perm = [(s, s ^ (1 << bit)) for s in range(n)]
        got = lax.ppermute(send, axis_name, perm=perm)
        low = jnp.stack([keep, got], axis=pos)
        high = jnp.stack([got, keep], axis=pos)
        held = jnp.where(mine == 0, low, high)
    by_source = held.reshape((n,) + tuple(rest))
    return jnp.concatenate([by_source[k] for k in range(n)], axis=concat_axis)


def per_device(hidden, out_weight, token_blocks, counts):
    vocab_here, columns_here = out_weight.shape
    n_vocab = lax.psum(1, "vocab")
    n_dp = lax.psum(1, "dp")
    n_tb = vocab_here // TB
    block_lists = token_blocks[0]
    block_counts = counts[0]
    n_blk = block_lists.shape[0]
    own_blocks = hidden.shape[0] // BB
    assert own_blocks == 1 and n_blk == n_dp
    me_dp = lax.axis_index("dp")
    own_counts = lax.dynamic_slice_in_dim(block_counts, me_dp, 1, 0)

    with jax.named_scope("hidden_spread"):
        row_slices = bruck_all_to_all(hidden, "vocab", n_vocab, split_axis=0, concat_axis=1)
        plane_rows = bruck_all_to_all(row_slices, "dp", n_dp, split_axis=1, concat_axis=0)
        gathered = doubling_all_gather(plane_rows, n_vocab)
        group = hidden.shape[0] // n_vocab
        beam_columns = (
            gathered.reshape(n_vocab, n_dp, group, columns_here)
            .transpose(1, 0, 2, 3)
            .reshape(n_dp * n_vocab * group, columns_here)
        )

    with jax.named_scope("dense_logits"):
        full = jnp.einsum(
            "bd,vd->bv", beam_columns, out_weight, preferred_element_type=jnp.float32
        )
        full4 = full.reshape(n_blk, BB, n_tb, TB)
        rows = jnp.arange(n_blk, dtype=jnp.int32)[:, None]
        picked = full4[rows, :, block_lists, :]

    logits = lax.psum_scatter(picked, "dp", scatter_dimension=0, tiled=True)

    with jax.named_scope("softmax_stats"):
        live = jnp.arange(MOST, dtype=jnp.int32)[None, :] < own_counts[:, None]
        live_mask = live[:, :, None, None]
        masked = jnp.where(live_mask, logits, -jnp.inf)
        local_max = jnp.max(masked, axis=(1, 3))
        local_total = jnp.sum(jnp.exp(masked - local_max[:, None, :, None]), axis=(1, 3))
        stats = lax.all_gather(jnp.stack([local_max, local_total]), "vocab", axis=0)
        beam_max = jnp.max(stats[:, 0], axis=0)
        beam_total = jnp.sum(stats[:, 1] * jnp.exp(stats[:, 0] - beam_max[None]), axis=0)
        shifted = logits - beam_max[:, None, :, None] - jnp.log(beam_total)[:, None, :, None]
        allowed_logprob = jnp.where(live_mask, shifted, 0.0)
        probabilities = jnp.where(live_mask, jnp.exp(shifted), 0.0).astype(jnp.bfloat16)

    prob_part = lax.all_gather(probabilities, "dp", axis=0, tiled=True)

    with jax.named_scope("dense_expected"):
        onehot = (
            block_lists[:, :, None] == jnp.arange(n_tb, dtype=jnp.int32)[None, None, :]
        ).astype(jnp.bfloat16)
        spread = jnp.einsum(
            "bsk,bsrt->brkt", onehot, prob_part, preferred_element_type=jnp.float32
        ).astype(jnp.bfloat16)
        embedding_part = jnp.einsum(
            "bv,vd->bd",
            spread.reshape(n_blk * BB, n_tb * TB),
            out_weight,
            preferred_element_type=jnp.float32,
        )
    summed = halving_reduce_scatter(embedding_part, n_vocab)
    squares = butterfly_sum(jnp.sum(summed * summed, axis=1), "dp", n_dp)
    width = hidden.shape[1] * n_vocab
    expected = summed * lax.rsqrt(squares / width + 1e-06)[:, None]
    return (allowed_logprob[None], expected)


def solution(mesh):
    in_specs = (P("dp", "vocab"), P("vocab", "dp"), P("vocab", None, None), P("vocab", None))
    out_specs = (P("vocab", "dp", None, None, None), P("vocab", "dp"))
    return jax.shard_map(
        per_device, mesh=mesh, in_specs=in_specs, out_specs=out_specs, check_vma=False
    )
```

```python
import jax
import jax.numpy as jnp
from jax import lax
from jax.sharding import PartitionSpec as P

TB = 128
BB = 128
MOST = 16


def exchange_stage(x, remaining, bit, n):
    me = lax.axis_index("vocab")
    axis = remaining.index(bit)
    mine = (me // (1 << bit)) % 2
    keep = lax.dynamic_index_in_dim(x, mine, axis=axis, keepdims=False)
    send = lax.dynamic_index_in_dim(x, 1 - mine, axis=axis, keepdims=False)
    perm = [(s, s ^ (1 << bit)) for s in range(n)]
    got = lax.ppermute(send, "vocab", perm=perm)
    return keep + got, [b for b in remaining if b != bit]


def halving_reduce_scatter(part, n):
    levels = n.bit_length() - 1
    rows, cols = part.shape
    group = rows // n
    remaining = list(range(levels - 1, -1, -1))
    x = part.reshape([2] * levels + [group, cols])
    with jax.named_scope("summed_core_stage"):
        x, remaining = exchange_stage(x, remaining, 0, n)
    half = cols // 2
    first, second = x[..., :half], x[..., half:]
    rest_a, rest_b = list(remaining), list(remaining)
    order_a = sorted(remaining)
    order_b = sorted(remaining, reverse=True)
    for step in range(len(order_a)):
        with jax.named_scope("summed_chip_stage"):
            first, rest_a = exchange_stage(first, rest_a, order_a[step], n)
            second, rest_b = exchange_stage(second, rest_b, order_b[step], n)
    return jnp.concatenate([first, second], axis=-1)


def gather_stage(x, have, bit, n):
    me = lax.axis_index("vocab")
    mine = (me // (1 << bit)) % 2
    perm = [(s, s ^ (1 << bit)) for s in range(n)]
    got = lax.ppermute(x, "vocab", perm=perm)
    pos = len([b for b in have if b > bit])
    low = jnp.stack([x, got], axis=pos)
    high = jnp.stack([got, x], axis=pos)
    return jnp.where(mine == 0, low, high), sorted(have + [bit], reverse=True)


def doubling_all_gather(x, n):
    levels = n.bit_length() - 1
    rows, cols = x.shape
    half = cols // 2
    first, second = x[:, :half], x[:, half:]
    have_a, have_b = [], []
    order_a = list(range(1, levels)) + [0]
    order_b = list(range(levels - 1, 0, -1)) + [0]
    for step in range(levels):
        with jax.named_scope("hidden_gather_stage"):
            first, have_a = gather_stage(first, have_a, order_a[step], n)
            second, have_b = gather_stage(second, have_b, order_b[step], n)
    joined = jnp.concatenate([first, second], axis=-1)
    return joined.reshape(n * rows, cols)


def bruck_all_to_all(x, axis_name, n, split_axis, concat_axis):
    me = lax.axis_index(axis_name)
    levels = n.bit_length() - 1
    shape = list(x.shape)
    shape[split_axis : split_axis + 1] = [n, x.shape[split_axis] // n]
    pieces = jnp.moveaxis(x.reshape(shape), split_axis, 0)
    rest = pieces.shape[1:]
    held = pieces.reshape([2] * levels + list(rest))
    for bit in range(levels):
        pos = levels - 1 - bit
        mine = (me // (1 << bit)) % 2
        keep = lax.dynamic_index_in_dim(held, mine, axis=pos, keepdims=False)
        send = lax.dynamic_index_in_dim(held, 1 - mine, axis=pos, keepdims=False)
        perm = [(s, s ^ (1 << bit)) for s in range(n)]
        got = lax.ppermute(send, axis_name, perm=perm)
        low = jnp.stack([keep, got], axis=pos)
        high = jnp.stack([got, keep], axis=pos)
        held = jnp.where(mine == 0, low, high)
    by_source = held.reshape((n,) + tuple(rest))
    return jnp.concatenate([by_source[k] for k in range(n)], axis=concat_axis)


def small_gather(x, axis_name, n):
    me = lax.axis_index(axis_name)
    got = [x]
    for shift in range(1, n):
        perm = [(s, (s + shift) % n) for s in range(n)]
        got.append(lax.ppermute(x, axis_name, perm=perm))
    order = (me - jnp.arange(n, dtype=jnp.int32)) % n
    return jnp.take(jnp.stack(got), order, axis=0)


def per_device(hidden, out_weight, token_blocks, counts):
    vocab_here, columns_here = out_weight.shape
    n_vocab = lax.psum(1, "vocab")
    n_dp = lax.psum(1, "dp")
    n_tb = vocab_here // TB
    block_lists = token_blocks[0]
    block_counts = counts[0]
    n_blk = block_lists.shape[0]
    own_blocks = hidden.shape[0] // BB
    assert own_blocks == 1 and n_blk == n_dp
    me_dp = lax.axis_index("dp")
    own_counts = lax.dynamic_slice_in_dim(block_counts, me_dp, 1, 0)

    with jax.named_scope("hidden_spread"):
        row_slices = bruck_all_to_all(hidden, "vocab", n_vocab, split_axis=0, concat_axis=1)
        plane_rows = bruck_all_to_all(row_slices, "dp", n_dp, split_axis=1, concat_axis=0)
        gathered = doubling_all_gather(plane_rows, n_vocab)
        group = hidden.shape[0] // n_vocab
        beam_columns = (
            gathered.reshape(n_vocab, n_dp, group, columns_here)
            .transpose(1, 0, 2, 3)
            .reshape(n_dp * n_vocab * group, columns_here)
        )

    with jax.named_scope("dense_logits"):
        full = jnp.einsum(
            "bd,vd->bv", beam_columns, out_weight, preferred_element_type=jnp.float32
        )
        full4 = full.reshape(n_blk, BB, n_tb, TB)
        rows = jnp.arange(n_blk, dtype=jnp.int32)[:, None]
        picked = full4[rows, :, block_lists, :]

    logits = lax.psum_scatter(picked, "dp", scatter_dimension=0, tiled=True)

    with jax.named_scope("softmax_stats"):
        live = jnp.arange(MOST, dtype=jnp.int32)[None, :] < own_counts[:, None]
        live_mask = live[:, :, None, None]
        masked = jnp.where(live_mask, logits, -jnp.inf)
        local_max = jnp.max(masked, axis=(1, 3))
        local_total = jnp.sum(jnp.exp(masked - local_max[:, None, :, None]), axis=(1, 3))
        stats = small_gather(jnp.stack([local_max, local_total]), "vocab", n_vocab)
        beam_max = jnp.max(stats[:, 0], axis=0)
        beam_total = jnp.sum(stats[:, 1] * jnp.exp(stats[:, 0] - beam_max[None]), axis=0)
        shifted = logits - beam_max[:, None, :, None] - jnp.log(beam_total)[:, None, :, None]
        allowed_logprob = jnp.where(live_mask, shifted, 0.0)
        probabilities = jnp.where(live_mask, jnp.exp(shifted), 0.0).astype(jnp.bfloat16)

    prob_part = lax.all_gather(probabilities, "dp", axis=0, tiled=True)

    with jax.named_scope("dense_expected"):
        onehot = (
            block_lists[:, :, None] == jnp.arange(n_tb, dtype=jnp.int32)[None, None, :]
        ).astype(jnp.bfloat16)
        spread = jnp.einsum(
            "bsk,bsrt->brkt", onehot, prob_part, preferred_element_type=jnp.float32
        ).astype(jnp.bfloat16)
        embedding_part = jnp.einsum(
            "bv,vd->bd",
            spread.reshape(n_blk * BB, n_tb * TB),
            out_weight,
            preferred_element_type=jnp.float32,
        )
    summed = halving_reduce_scatter(embedding_part, n_vocab)
    squares = jnp.sum(small_gather(jnp.sum(summed * summed, axis=1), "dp", n_dp), axis=0)
    width = hidden.shape[1] * n_vocab
    expected = summed * lax.rsqrt(squares / width + 1e-06)[:, None]
    return (allowed_logprob[None], expected)


def solution(mesh):
    in_specs = (P("dp", "vocab"), P("vocab", "dp"), P("vocab", None, None), P("vocab", None))
    out_specs = (P("vocab", "dp", None, None, None), P("vocab", "dp"))
    return jax.shard_map(
        per_device, mesh=mesh, in_specs=in_specs, out_specs=out_specs, check_vma=False
    )
```

```python
import jax
import jax.numpy as jnp
from jax import lax
from jax.sharding import PartitionSpec as P

TB = 128
BB = 128
MOST = 16


def exchange_stage(x, remaining, bit, n):
    me = lax.axis_index("vocab")
    axis = remaining.index(bit)
    mine = (me // (1 << bit)) % 2
    keep = lax.dynamic_index_in_dim(x, mine, axis=axis, keepdims=False)
    send = lax.dynamic_index_in_dim(x, 1 - mine, axis=axis, keepdims=False)
    perm = [(s, s ^ (1 << bit)) for s in range(n)]
    got = lax.ppermute(send, "vocab", perm=perm)
    return keep + got, [b for b in remaining if b != bit]


def halving_reduce_scatter(keep, send, n):
    levels = n.bit_length() - 1
    _, group, cols = keep.shape
    perm = [(s, s ^ 1) for s in range(n)]
    with jax.named_scope("summed_core_stage"):
        x = keep + lax.ppermute(send, "vocab", perm=perm)
    x = x.reshape([2] * (levels - 1) + [group, cols])
    remaining = list(range(levels - 1, 0, -1))
    half = cols // 2
    first, second = x[..., :half], x[..., half:]
    rest_a, rest_b = list(remaining), list(remaining)
    order_a = sorted(remaining)
    order_b = sorted(remaining, reverse=True)
    for step in range(len(order_a)):
        with jax.named_scope("summed_chip_stage"):
            first, rest_a = exchange_stage(first, rest_a, order_a[step], n)
            second, rest_b = exchange_stage(second, rest_b, order_b[step], n)
    return jnp.concatenate([first, second], axis=-1)


def gather_stage(x, have, bit, n):
    me = lax.axis_index("vocab")
    mine = (me // (1 << bit)) % 2
    perm = [(s, s ^ (1 << bit)) for s in range(n)]
    got = lax.ppermute(x, "vocab", perm=perm)
    pos = len([b for b in have if b > bit])
    low = jnp.stack([x, got], axis=pos)
    high = jnp.stack([got, x], axis=pos)
    return jnp.where(mine == 0, low, high), sorted(have + [bit], reverse=True)


def doubling_all_gather(x, n):
    levels = n.bit_length() - 1
    rows, cols = x.shape
    half = cols // 2
    first, second = x[:, :half], x[:, half:]
    have_a, have_b = [], []
    order_a = list(range(1, levels)) + [0]
    order_b = list(range(levels - 1, 0, -1)) + [0]
    for step in range(levels):
        with jax.named_scope("hidden_gather_stage"):
            first, have_a = gather_stage(first, have_a, order_a[step], n)
            second, have_b = gather_stage(second, have_b, order_b[step], n)
    joined = jnp.concatenate([first, second], axis=-1)
    return joined.reshape(n * rows, cols)


def butterfly_sum(x, axis_name, n):
    levels = n.bit_length() - 1
    for bit in range(levels):
        perm = [(s, s ^ (1 << bit)) for s in range(n)]
        x = x + lax.ppermute(x, axis_name, perm=perm)
    return x


def bruck_all_to_all(x, axis_name, n, split_axis, concat_axis):
    me = lax.axis_index(axis_name)
    levels = n.bit_length() - 1
    shape = list(x.shape)
    shape[split_axis : split_axis + 1] = [n, x.shape[split_axis] // n]
    pieces = jnp.moveaxis(x.reshape(shape), split_axis, 0)
    rest = pieces.shape[1:]
    held = pieces.reshape([2] * levels + list(rest))
    for bit in range(levels):
        pos = levels - 1 - bit
        mine = (me // (1 << bit)) % 2
        keep = lax.dynamic_index_in_dim(held, mine, axis=pos, keepdims=False)
        send = lax.dynamic_index_in_dim(held, 1 - mine, axis=pos, keepdims=False)
        perm = [(s, s ^ (1 << bit)) for s in range(n)]
        got = lax.ppermute(send, axis_name, perm=perm)
        low = jnp.stack([keep, got], axis=pos)
        high = jnp.stack([got, keep], axis=pos)
        held = jnp.where(mine == 0, low, high)
    by_source = held.reshape((n,) + tuple(rest))
    return jnp.concatenate([by_source[k] for k in range(n)], axis=concat_axis)


def per_device(hidden, out_weight, token_blocks, counts):
    vocab_here, columns_here = out_weight.shape
    n_vocab = lax.psum(1, "vocab")
    n_dp = lax.psum(1, "dp")
    n_tb = vocab_here // TB
    block_lists = token_blocks[0]
    block_counts = counts[0]
    n_blk = block_lists.shape[0]
    own_blocks = hidden.shape[0] // BB
    assert own_blocks == 1 and n_blk == n_dp
    me_dp = lax.axis_index("dp")
    own_counts = lax.dynamic_slice_in_dim(block_counts, me_dp, 1, 0)

    with jax.named_scope("hidden_spread"):
        row_slices = bruck_all_to_all(hidden, "vocab", n_vocab, split_axis=0, concat_axis=1)
        plane_rows = bruck_all_to_all(row_slices, "dp", n_dp, split_axis=1, concat_axis=0)
        gathered = doubling_all_gather(plane_rows, n_vocab)
        group = hidden.shape[0] // n_vocab
        beam_columns = (
            gathered.reshape(n_vocab, n_dp, group, columns_here)
            .transpose(1, 0, 2, 3)
            .reshape(n_dp * n_vocab * group, columns_here)
        )

    with jax.named_scope("dense_logits"):
        full = jnp.einsum(
            "bd,vd->bv", beam_columns, out_weight, preferred_element_type=jnp.float32
        )
        full4 = full.reshape(n_blk, BB, n_tb, TB)
        rows = jnp.arange(n_blk, dtype=jnp.int32)[:, None]
        picked = full4[rows, :, block_lists, :]

    logits = lax.psum_scatter(picked, "dp", scatter_dimension=0, tiled=True)

    with jax.named_scope("softmax_stats"):
        live = jnp.arange(MOST, dtype=jnp.int32)[None, :] < own_counts[:, None]
        live_mask = live[:, :, None, None]
        masked = jnp.where(live_mask, logits, -jnp.inf)
        local_max = jnp.max(masked, axis=(1, 3))
        local_total = jnp.sum(jnp.exp(masked - local_max[:, None, :, None]), axis=(1, 3))
        stats = lax.all_gather(jnp.stack([local_max, local_total]), "vocab", axis=0)
        beam_max = jnp.max(stats[:, 0], axis=0)
        beam_total = jnp.sum(stats[:, 1] * jnp.exp(stats[:, 0] - beam_max[None]), axis=0)
        shifted = logits - beam_max[:, None, :, None] - jnp.log(beam_total)[:, None, :, None]
        allowed_logprob = jnp.where(live_mask, shifted, 0.0)
        probabilities = jnp.where(live_mask, jnp.exp(shifted), 0.0).astype(jnp.bfloat16)

    prob_part = lax.all_gather(probabilities, "dp", axis=0, tiled=True)

    rows_per_dev = n_blk * BB // n_vocab
    pairs = BB // rows_per_dev // 2
    onehot = (
        block_lists[:, :, None] == jnp.arange(n_tb, dtype=jnp.int32)[None, None, :]
    ).astype(jnp.bfloat16)
    halves = prob_part.reshape(n_blk, MOST, pairs, 2, rows_per_dev, TB)
    low_bit = lax.axis_index("vocab") % 2

    def expected_half(which):
        with jax.named_scope("dense_expected"):
            chosen = lax.dynamic_index_in_dim(halves, which, axis=3, keepdims=False)
            chosen = chosen.reshape(n_blk, MOST, pairs * rows_per_dev, TB)
            spread = jnp.einsum(
                "bsk,bsrt->brkt", onehot, chosen, preferred_element_type=jnp.float32
            ).astype(jnp.bfloat16)
            term = jnp.einsum(
                "brkt,ktd->brd",
                spread,
                out_weight.reshape(n_tb, TB, columns_here),
                preferred_element_type=jnp.float32,
            )
            return term.reshape(n_blk * pairs, rows_per_dev, columns_here)

    send_half = expected_half(1 - low_bit)
    keep_half = expected_half(low_bit)
    summed = halving_reduce_scatter(keep_half, send_half, n_vocab)
    squares = butterfly_sum(jnp.sum(summed * summed, axis=1), "dp", n_dp)
    width = hidden.shape[1] * n_vocab
    expected = summed * lax.rsqrt(squares / width + 1e-06)[:, None]
    return (allowed_logprob[None], expected)


def solution(mesh):
    in_specs = (P("dp", "vocab"), P("vocab", "dp"), P("vocab", None, None), P("vocab", None))
    out_specs = (P("vocab", "dp", None, None, None), P("vocab", "dp"))
    return jax.shard_map(
        per_device, mesh=mesh, in_specs=in_specs, out_specs=out_specs, check_vma=False
    )
```

```python
import jax
import jax.numpy as jnp
from jax import lax
from jax.sharding import PartitionSpec as P

TB = 128
BB = 128
MOST = 16


def exchange_stage(x, remaining, bit, n):
    me = lax.axis_index("vocab")
    axis = remaining.index(bit)
    mine = (me // (1 << bit)) % 2
    keep = lax.dynamic_index_in_dim(x, mine, axis=axis, keepdims=False)
    send = lax.dynamic_index_in_dim(x, 1 - mine, axis=axis, keepdims=False)
    perm = [(s, s ^ (1 << bit)) for s in range(n)]
    got = lax.ppermute(send, "vocab", perm=perm)
    return keep + got, [b for b in remaining if b != bit]


def halving_reduce_scatter(keep, send, n):
    levels = n.bit_length() - 1
    _, group, cols = keep.shape
    perm = [(s, s ^ 1) for s in range(n)]
    with jax.named_scope("summed_core_stage"):
        x = keep + lax.ppermute(send, "vocab", perm=perm)
    x = x.reshape([2] * (levels - 1) + [group, cols])
    remaining = list(range(levels - 1, 0, -1))
    half = cols // 2
    first, second = x[..., :half], x[..., half:]
    rest_a, rest_b = list(remaining), list(remaining)
    order_a = sorted(remaining)
    order_b = sorted(remaining, reverse=True)
    for step in range(len(order_a)):
        with jax.named_scope("summed_chip_stage"):
            first, rest_a = exchange_stage(first, rest_a, order_a[step], n)
            second, rest_b = exchange_stage(second, rest_b, order_b[step], n)
    return jnp.concatenate([first, second], axis=-1)


def gather_stage(x, have, bit, n):
    me = lax.axis_index("vocab")
    mine = (me // (1 << bit)) % 2
    perm = [(s, s ^ (1 << bit)) for s in range(n)]
    got = lax.ppermute(x, "vocab", perm=perm)
    pos = len([b for b in have if b > bit])
    low = jnp.stack([x, got], axis=pos)
    high = jnp.stack([got, x], axis=pos)
    return jnp.where(mine == 0, low, high), sorted(have + [bit], reverse=True)


def doubling_all_gather(x, n):
    levels = n.bit_length() - 1
    rows, cols = x.shape
    half = cols // 2
    first, second = x[:, :half], x[:, half:]
    have_a, have_b = [], []
    order_a = list(range(1, levels)) + [0]
    order_b = list(range(levels - 1, 0, -1)) + [0]
    for step in range(levels):
        with jax.named_scope("hidden_gather_stage"):
            first, have_a = gather_stage(first, have_a, order_a[step], n)
            second, have_b = gather_stage(second, have_b, order_b[step], n)
    joined = jnp.concatenate([first, second], axis=-1)
    return joined.reshape(n * rows, cols)


def butterfly_sum(x, axis_name, n):
    levels = n.bit_length() - 1
    for bit in range(levels):
        perm = [(s, s ^ (1 << bit)) for s in range(n)]
        x = x + lax.ppermute(x, axis_name, perm=perm)
    return x


def bruck_all_to_all(x, axis_name, n, split_axis, concat_axis):
    me = lax.axis_index(axis_name)
    levels = n.bit_length() - 1
    shape = list(x.shape)
    shape[split_axis : split_axis + 1] = [n, x.shape[split_axis] // n]
    pieces = jnp.moveaxis(x.reshape(shape), split_axis, 0)
    rest = pieces.shape[1:]
    held = pieces.reshape([2] * levels + list(rest))
    for bit in range(levels):
        pos = levels - 1 - bit
        mine = (me // (1 << bit)) % 2
        keep = lax.dynamic_index_in_dim(held, mine, axis=pos, keepdims=False)
        send = lax.dynamic_index_in_dim(held, 1 - mine, axis=pos, keepdims=False)
        perm = [(s, s ^ (1 << bit)) for s in range(n)]
        got = lax.ppermute(send, axis_name, perm=perm)
        low = jnp.stack([keep, got], axis=pos)
        high = jnp.stack([got, keep], axis=pos)
        held = jnp.where(mine == 0, low, high)
    by_source = held.reshape((n,) + tuple(rest))
    return jnp.concatenate([by_source[k] for k in range(n)], axis=concat_axis)


def direct_spread(hidden, n_vocab, n_dp):
    rows, chunk = hidden.shape
    per_slice = n_vocab // n_dp
    group = rows // n_vocab
    me_v = lax.axis_index("vocab")
    me_d = lax.axis_index("dp")
    pieces = hidden.reshape(n_vocab, group, chunk)
    got = []
    for shift in range(n_vocab):
        target = (me_v % per_slice + per_slice * me_d + shift) % n_vocab
        send = lax.dynamic_index_in_dim(pieces, target, axis=0, keepdims=False)
        perm = []
        for d in range(n_dp):
            for v in range(n_vocab):
                k = (v % per_slice + per_slice * d + shift) % n_vocab
                perm.append((d * n_vocab + v, (v // per_slice) * n_vocab + k))
        got.append(lax.ppermute(send, ("dp", "vocab"), perm=perm))
    received = jnp.stack(got)
    slot = jnp.arange(n_vocab, dtype=jnp.int32)
    order = (me_v - slot) % n_vocab
    placed = jnp.take(received, order, axis=0)
    placed = placed.reshape(n_dp, per_slice, group, chunk).transpose(0, 2, 1, 3)
    return placed.reshape(n_dp * group, per_slice * chunk)


def per_device(hidden, out_weight, token_blocks, counts):
    vocab_here, columns_here = out_weight.shape
    n_vocab = lax.psum(1, "vocab")
    n_dp = lax.psum(1, "dp")
    n_tb = vocab_here // TB
    block_lists = token_blocks[0]
    block_counts = counts[0]
    n_blk = block_lists.shape[0]
    own_blocks = hidden.shape[0] // BB
    assert own_blocks == 1 and n_blk == n_dp
    me_dp = lax.axis_index("dp")
    own_counts = lax.dynamic_slice_in_dim(block_counts, me_dp, 1, 0)

    with jax.named_scope("hidden_spread"):
        plane_rows = direct_spread(hidden, n_vocab, n_dp)
        gathered = doubling_all_gather(plane_rows, n_vocab)
        group = hidden.shape[0] // n_vocab
        beam_columns = (
            gathered.reshape(n_vocab, n_dp, group, columns_here)
            .transpose(1, 0, 2, 3)
            .reshape(n_dp * n_vocab * group, columns_here)
        )

    with jax.named_scope("dense_logits"):
        full = jnp.einsum(
            "bd,vd->bv", beam_columns, out_weight, preferred_element_type=jnp.float32
        )
        full4 = full.reshape(n_blk, BB, n_tb, TB)
        rows = jnp.arange(n_blk, dtype=jnp.int32)[:, None]
        picked = full4[rows, :, block_lists, :]

    logits = lax.psum_scatter(picked, "dp", scatter_dimension=0, tiled=True)

    with jax.named_scope("softmax_stats"):
        live = jnp.arange(MOST, dtype=jnp.int32)[None, :] < own_counts[:, None]
        live_mask = live[:, :, None, None]
        masked = jnp.where(live_mask, logits, -jnp.inf)
        local_max = jnp.max(masked, axis=(1, 3))
        local_total = jnp.sum(jnp.exp(masked - local_max[:, None, :, None]), axis=(1, 3))
        stats = lax.all_gather(jnp.stack([local_max, local_total]), "vocab", axis=0)
        beam_max = jnp.max(stats[:, 0], axis=0)
        beam_total = jnp.sum(stats[:, 1] * jnp.exp(stats[:, 0] - beam_max[None]), axis=0)
        shifted = logits - beam_max[:, None, :, None] - jnp.log(beam_total)[:, None, :, None]
        allowed_logprob = jnp.where(live_mask, shifted, 0.0)
        probabilities = jnp.where(live_mask, jnp.exp(shifted), 0.0).astype(jnp.bfloat16)

    prob_part = lax.all_gather(probabilities, "dp", axis=0, tiled=True)

    rows_per_dev = n_blk * BB // n_vocab
    pairs = BB // rows_per_dev // 2
    onehot = (
        block_lists[:, :, None] == jnp.arange(n_tb, dtype=jnp.int32)[None, None, :]
    ).astype(jnp.bfloat16)
    halves = prob_part.reshape(n_blk, MOST, pairs, 2, rows_per_dev, TB)
    low_bit = lax.axis_index("vocab") % 2

    def expected_half(which):
        with jax.named_scope("dense_expected"):
            chosen = lax.dynamic_index_in_dim(halves, which, axis=3, keepdims=False)
            chosen = chosen.reshape(n_blk, MOST, pairs * rows_per_dev, TB)
            spread = jnp.einsum(
                "bsk,bsrt->brkt", onehot, chosen, preferred_element_type=jnp.float32
            ).astype(jnp.bfloat16)
            term = jnp.einsum(
                "brkt,ktd->brd",
                spread,
                out_weight.reshape(n_tb, TB, columns_here),
                preferred_element_type=jnp.float32,
            )
            return term.reshape(n_blk * pairs, rows_per_dev, columns_here)

    send_half = expected_half(1 - low_bit)
    keep_half = expected_half(low_bit)
    summed = halving_reduce_scatter(keep_half, send_half, n_vocab)
    squares = butterfly_sum(jnp.sum(summed * summed, axis=1), "dp", n_dp)
    width = hidden.shape[1] * n_vocab
    expected = summed * lax.rsqrt(squares / width + 1e-06)[:, None]
    return (allowed_logprob[None], expected)


def solution(mesh):
    in_specs = (P("dp", "vocab"), P("vocab", "dp"), P("vocab", None, None), P("vocab", None))
    out_specs = (P("vocab", "dp", None, None, None), P("vocab", "dp"))
    return jax.shard_map(
        per_device, mesh=mesh, in_specs=in_specs, out_specs=out_specs, check_vma=False
    )
```

```python
import jax
import jax.numpy as jnp
from jax import lax
from jax.sharding import PartitionSpec as P

TB = 128
BB = 128
MOST = 16


def exchange_stage(x, remaining, bit, n):
    me = lax.axis_index("vocab")
    axis = remaining.index(bit)
    mine = (me // (1 << bit)) % 2
    keep = lax.dynamic_index_in_dim(x, mine, axis=axis, keepdims=False)
    send = lax.dynamic_index_in_dim(x, 1 - mine, axis=axis, keepdims=False)
    perm = [(s, s ^ (1 << bit)) for s in range(n)]
    got = lax.ppermute(send, "vocab", perm=perm)
    return keep + got, [b for b in remaining if b != bit]


def halving_reduce_scatter(keep, send, n):
    levels = n.bit_length() - 1
    _, group, cols = keep.shape
    perm = [(s, s ^ 1) for s in range(n)]
    with jax.named_scope("summed_core_stage"):
        x = keep + lax.ppermute(send, "vocab", perm=perm)
    x = x.reshape([2] * (levels - 1) + [group, cols])
    remaining = list(range(levels - 1, 0, -1))
    half = cols // 2
    first, second = x[..., :half], x[..., half:]
    rest_a, rest_b = list(remaining), list(remaining)
    order_a = sorted(remaining)
    order_b = sorted(remaining, reverse=True)
    for step in range(len(order_a)):
        with jax.named_scope("summed_chip_stage"):
            first, rest_a = exchange_stage(first, rest_a, order_a[step], n)
            second, rest_b = exchange_stage(second, rest_b, order_b[step], n)
    return jnp.concatenate([first, second], axis=-1)


def gather_stage(x, have, bit, n):
    me = lax.axis_index("vocab")
    mine = (me // (1 << bit)) % 2
    perm = [(s, s ^ (1 << bit)) for s in range(n)]
    got = lax.ppermute(x, "vocab", perm=perm)
    pos = len([b for b in have if b > bit])
    low = jnp.stack([x, got], axis=pos)
    high = jnp.stack([got, x], axis=pos)
    return jnp.where(mine == 0, low, high), sorted(have + [bit], reverse=True)


def doubling_all_gather(x, n):
    levels = n.bit_length() - 1
    rows, cols = x.shape
    half = cols // 2
    first, second = x[:, :half], x[:, half:]
    have_a, have_b = [], []
    order_a = list(range(1, levels)) + [0]
    order_b = list(range(levels - 1, 0, -1)) + [0]
    for step in range(levels):
        with jax.named_scope("hidden_gather_stage"):
            first, have_a = gather_stage(first, have_a, order_a[step], n)
            second, have_b = gather_stage(second, have_b, order_b[step], n)
    joined = jnp.concatenate([first, second], axis=-1)
    return joined.reshape(n * rows, cols)


def butterfly_sum(x, axis_name, n):
    levels = n.bit_length() - 1
    for bit in range(levels):
        perm = [(s, s ^ (1 << bit)) for s in range(n)]
        x = x + lax.ppermute(x, axis_name, perm=perm)
    return x


def bruck_all_to_all(x, axis_name, n, split_axis, concat_axis):
    me = lax.axis_index(axis_name)
    levels = n.bit_length() - 1
    shape = list(x.shape)
    shape[split_axis : split_axis + 1] = [n, x.shape[split_axis] // n]
    pieces = jnp.moveaxis(x.reshape(shape), split_axis, 0)
    rest = pieces.shape[1:]
    held = pieces.reshape([2] * levels + list(rest))
    for bit in range(levels):
        pos = levels - 1 - bit
        mine = (me // (1 << bit)) % 2
        keep = lax.dynamic_index_in_dim(held, mine, axis=pos, keepdims=False)
        send = lax.dynamic_index_in_dim(held, 1 - mine, axis=pos, keepdims=False)
        perm = [(s, s ^ (1 << bit)) for s in range(n)]
        got = lax.ppermute(send, axis_name, perm=perm)
        low = jnp.stack([keep, got], axis=pos)
        high = jnp.stack([got, keep], axis=pos)
        held = jnp.where(mine == 0, low, high)
    by_source = held.reshape((n,) + tuple(rest))
    return jnp.concatenate([by_source[k] for k in range(n)], axis=concat_axis)


def direct_spread(hidden, n_vocab, n_dp):
    rows, chunk = hidden.shape
    per_slice = n_vocab // n_dp
    group = rows // n_vocab
    me_v = lax.axis_index("vocab")
    me_d = lax.axis_index("dp")
    pieces = hidden.reshape(n_vocab, group, chunk)
    got = []
    for shift in range(n_vocab):
        target = (me_v % per_slice + per_slice * me_d + shift) % n_vocab
        send = lax.dynamic_index_in_dim(pieces, target, axis=0, keepdims=False)
        perm = []
        for d in range(n_dp):
            for v in range(n_vocab):
                k = (v % per_slice + per_slice * d + shift) % n_vocab
                perm.append((d * n_vocab + v, (v // per_slice) * n_vocab + k))
        got.append(lax.ppermute(send, ("dp", "vocab"), perm=perm))
    received = jnp.stack(got)
    slot = jnp.arange(n_vocab, dtype=jnp.int32)
    order = (me_v - slot) % n_vocab
    placed = jnp.take(received, order, axis=0)
    placed = placed.reshape(n_dp, per_slice, group, chunk).transpose(0, 2, 1, 3)
    return placed.reshape(n_dp * group, per_slice * chunk)


def line_reduce_scatter(partials, n):
    me = lax.axis_index("dp")
    own = lambda block: lax.dynamic_index_in_dim(
        partials, jnp.clip(block, 0, n - 1), axis=0, keepdims=False
    )
    from_left = None
    from_right = None
    for step in range(1, n):
        send_up = own(me + n - step)
        send_down = own(me - n + step)
        if from_left is not None:
            send_up = send_up + from_left
            send_down = send_down + from_right
        send_up, send_down = lax.optimization_barrier((send_up, send_down))
        upward = [(s, s + 1) for s in range(0, step)]
        downward = [(s, s - 1) for s in range(n - step, n)]
        from_left = lax.ppermute(send_up, "dp", perm=upward)
        from_right = lax.ppermute(send_down, "dp", perm=downward)
    return (own(me) + from_left + from_right)[None]


def line_all_gather(own_part, n):
    me = lax.axis_index("dp")
    got = [own_part]
    from_left, from_right = own_part, own_part
    for step in range(1, n):
        upward = [(s, s + 1) for s in range(step - 1, n - 1)]
        downward = [(s, s - 1) for s in range(1, n - step + 1)]
        from_left, from_right = lax.optimization_barrier((from_left, from_right))
        from_left = lax.ppermute(from_left, "dp", perm=upward)
        from_right = lax.ppermute(from_right, "dp", perm=downward)
        got += [from_left, from_right]
    blocks = []
    for block in range(n):
        pick = jnp.where(me == block, got[0], jnp.zeros_like(got[0]))
        for step in range(1, n):
            pick = jnp.where(me - step == block, got[2 * step - 1], pick)
            pick = jnp.where(me + step == block, got[2 * step], pick)
        blocks.append(pick)
    return jnp.stack(blocks)


def per_device(hidden, out_weight, token_blocks, counts):
    vocab_here, columns_here = out_weight.shape
    n_vocab = lax.psum(1, "vocab")
    n_dp = lax.psum(1, "dp")
    n_tb = vocab_here // TB
    block_lists = token_blocks[0]
    block_counts = counts[0]
    n_blk = block_lists.shape[0]
    own_blocks = hidden.shape[0] // BB
    assert own_blocks == 1 and n_blk == n_dp
    me_dp = lax.axis_index("dp")
    own_counts = lax.dynamic_slice_in_dim(block_counts, me_dp, 1, 0)

    with jax.named_scope("hidden_spread"):
        plane_rows = direct_spread(hidden, n_vocab, n_dp)
        gathered = doubling_all_gather(plane_rows, n_vocab)
        group = hidden.shape[0] // n_vocab
        beam_columns = (
            gathered.reshape(n_vocab, n_dp, group, columns_here)
            .transpose(1, 0, 2, 3)
            .reshape(n_dp * n_vocab * group, columns_here)
        )

    with jax.named_scope("dense_logits"):
        full = jnp.einsum(
            "bd,vd->bv", beam_columns, out_weight, preferred_element_type=jnp.float32
        )
        full4 = full.reshape(n_blk, BB, n_tb, TB)
        rows = jnp.arange(n_blk, dtype=jnp.int32)[:, None]
        picked = full4[rows, :, block_lists, :]

    with jax.named_scope("logits_line_reduce"):
        logits = line_reduce_scatter(picked, n_dp)

    with jax.named_scope("softmax_stats"):
        live = jnp.arange(MOST, dtype=jnp.int32)[None, :] < own_counts[:, None]
        live_mask = live[:, :, None, None]
        masked = jnp.where(live_mask, logits, -jnp.inf)
        local_max = jnp.max(masked, axis=(1, 3))
        local_total = jnp.sum(jnp.exp(masked - local_max[:, None, :, None]), axis=(1, 3))
        stats = lax.all_gather(jnp.stack([local_max, local_total]), "vocab", axis=0)
        beam_max = jnp.max(stats[:, 0], axis=0)
        beam_total = jnp.sum(stats[:, 1] * jnp.exp(stats[:, 0] - beam_max[None]), axis=0)
        shifted = logits - beam_max[:, None, :, None] - jnp.log(beam_total)[:, None, :, None]
        allowed_logprob = jnp.where(live_mask, shifted, 0.0)
        probabilities = jnp.where(live_mask, jnp.exp(shifted), 0.0).astype(jnp.bfloat16)

    prob_part = lax.all_gather(probabilities, "dp", axis=0, tiled=True)

    rows_per_dev = n_blk * BB // n_vocab
    pairs = BB // rows_per_dev // 2
    onehot = (
        block_lists[:, :, None] == jnp.arange(n_tb, dtype=jnp.int32)[None, None, :]
    ).astype(jnp.bfloat16)
    halves = prob_part.reshape(n_blk, MOST, pairs, 2, rows_per_dev, TB)
    low_bit = lax.axis_index("vocab") % 2

    def expected_half(which):
        with jax.named_scope("dense_expected"):
            chosen = lax.dynamic_index_in_dim(halves, which, axis=3, keepdims=False)
            chosen = chosen.reshape(n_blk, MOST, pairs * rows_per_dev, TB)
            spread = jnp.einsum(
                "bsk,bsrt->brkt", onehot, chosen, preferred_element_type=jnp.float32
            ).astype(jnp.bfloat16)
            term = jnp.einsum(
                "brkt,ktd->brd",
                spread,
                out_weight.reshape(n_tb, TB, columns_here),
                preferred_element_type=jnp.float32,
            )
            return term.reshape(n_blk * pairs, rows_per_dev, columns_here)

    send_half = expected_half(1 - low_bit)
    keep_half = expected_half(low_bit)
    summed = halving_reduce_scatter(keep_half, send_half, n_vocab)
    squares = butterfly_sum(jnp.sum(summed * summed, axis=1), "dp", n_dp)
    width = hidden.shape[1] * n_vocab
    expected = summed * lax.rsqrt(squares / width + 1e-06)[:, None]
    return (allowed_logprob[None], expected)


def solution(mesh):
    in_specs = (P("dp", "vocab"), P("vocab", "dp"), P("vocab", None, None), P("vocab", None))
    out_specs = (P("vocab", "dp", None, None, None), P("vocab", "dp"))
    return jax.shard_map(
        per_device, mesh=mesh, in_specs=in_specs, out_specs=out_specs, check_vma=False
    )
```

```python
import jax
import jax.numpy as jnp
from jax import lax
from jax.sharding import PartitionSpec as P

TB = 128
BB = 128
MOST = 16


def exchange_stage(x, remaining, bit, n):
    me = lax.axis_index("vocab")
    axis = remaining.index(bit)
    mine = (me // (1 << bit)) % 2
    keep = lax.dynamic_index_in_dim(x, mine, axis=axis, keepdims=False)
    send = lax.dynamic_index_in_dim(x, 1 - mine, axis=axis, keepdims=False)
    perm = [(s, s ^ (1 << bit)) for s in range(n)]
    got = lax.ppermute(send, "vocab", perm=perm)
    return keep + got, [b for b in remaining if b != bit]


def halving_reduce_scatter(keep, send, n):
    levels = n.bit_length() - 1
    _, group, cols = keep.shape
    perm = [(s, s ^ 1) for s in range(n)]
    with jax.named_scope("summed_core_stage"):
        x = keep + lax.ppermute(send, "vocab", perm=perm)
    x = x.reshape([2] * (levels - 1) + [group, cols])
    remaining = list(range(levels - 1, 0, -1))
    half = cols // 2
    first, second = x[..., :half], x[..., half:]
    rest_a, rest_b = list(remaining), list(remaining)
    order_a = sorted(remaining)
    order_b = sorted(remaining, reverse=True)
    for step in range(len(order_a)):
        with jax.named_scope("summed_chip_stage"):
            first, rest_a = exchange_stage(first, rest_a, order_a[step], n)
            second, rest_b = exchange_stage(second, rest_b, order_b[step], n)
    return jnp.concatenate([first, second], axis=-1)


def gather_stage(x, have, bit, n):
    me = lax.axis_index("vocab")
    mine = (me // (1 << bit)) % 2
    perm = [(s, s ^ (1 << bit)) for s in range(n)]
    got = lax.ppermute(x, "vocab", perm=perm)
    pos = len([b for b in have if b > bit])
    low = jnp.stack([x, got], axis=pos)
    high = jnp.stack([got, x], axis=pos)
    return jnp.where(mine == 0, low, high), sorted(have + [bit], reverse=True)


def doubling_all_gather(x, n):
    levels = n.bit_length() - 1
    rows, cols = x.shape
    half = cols // 2
    first, second = x[:, :half], x[:, half:]
    have_a, have_b = [], []
    order_a = list(range(1, levels)) + [0]
    order_b = list(range(levels - 1, 0, -1)) + [0]
    for step in range(levels):
        with jax.named_scope("hidden_gather_stage"):
            first, have_a = gather_stage(first, have_a, order_a[step], n)
            second, have_b = gather_stage(second, have_b, order_b[step], n)
    joined = jnp.concatenate([first, second], axis=-1)
    return joined.reshape(n * rows, cols)


def butterfly_sum(x, axis_name, n):
    levels = n.bit_length() - 1
    for bit in range(levels):
        perm = [(s, s ^ (1 << bit)) for s in range(n)]
        x = x + lax.ppermute(x, axis_name, perm=perm)
    return x


def bruck_all_to_all(x, axis_name, n, split_axis, concat_axis):
    me = lax.axis_index(axis_name)
    levels = n.bit_length() - 1
    shape = list(x.shape)
    shape[split_axis : split_axis + 1] = [n, x.shape[split_axis] // n]
    pieces = jnp.moveaxis(x.reshape(shape), split_axis, 0)
    rest = pieces.shape[1:]
    held = pieces.reshape([2] * levels + list(rest))
    for bit in range(levels):
        pos = levels - 1 - bit
        mine = (me // (1 << bit)) % 2
        keep = lax.dynamic_index_in_dim(held, mine, axis=pos, keepdims=False)
        send = lax.dynamic_index_in_dim(held, 1 - mine, axis=pos, keepdims=False)
        perm = [(s, s ^ (1 << bit)) for s in range(n)]
        got = lax.ppermute(send, axis_name, perm=perm)
        low = jnp.stack([keep, got], axis=pos)
        high = jnp.stack([got, keep], axis=pos)
        held = jnp.where(mine == 0, low, high)
    by_source = held.reshape((n,) + tuple(rest))
    return jnp.concatenate([by_source[k] for k in range(n)], axis=concat_axis)


def direct_spread(hidden, n_vocab, n_dp):
    rows, chunk = hidden.shape
    per_slice = n_vocab // n_dp
    group = rows // n_vocab
    me_v = lax.axis_index("vocab")
    me_d = lax.axis_index("dp")
    pieces = hidden.reshape(n_vocab, group, chunk)
    got = []
    for shift in range(n_vocab):
        target = (me_v % per_slice + per_slice * me_d + shift) % n_vocab
        send = lax.dynamic_index_in_dim(pieces, target, axis=0, keepdims=False)
        perm = []
        for d in range(n_dp):
            for v in range(n_vocab):
                k = (v % per_slice + per_slice * d + shift) % n_vocab
                perm.append((d * n_vocab + v, (v // per_slice) * n_vocab + k))
        got.append(lax.ppermute(send, ("dp", "vocab"), perm=perm))
    received = jnp.stack(got)
    slot = jnp.arange(n_vocab, dtype=jnp.int32)
    order = (me_v - slot) % n_vocab
    placed = jnp.take(received, order, axis=0)
    placed = placed.reshape(n_dp, per_slice, group, chunk).transpose(0, 2, 1, 3)
    return placed.reshape(n_dp * group, per_slice * chunk)


def per_device(hidden, out_weight, token_blocks, counts):
    vocab_here, columns_here = out_weight.shape
    n_vocab = lax.psum(1, "vocab")
    n_dp = lax.psum(1, "dp")
    n_tb = vocab_here // TB
    block_lists = token_blocks[0]
    block_counts = counts[0]
    n_blk = block_lists.shape[0]
    own_blocks = hidden.shape[0] // BB
    assert own_blocks == 1 and n_blk == n_dp
    me_dp = lax.axis_index("dp")
    own_counts = lax.dynamic_slice_in_dim(block_counts, me_dp, 1, 0)

    with jax.named_scope("hidden_spread"):
        plane_rows = direct_spread(hidden, n_vocab, n_dp)
        gathered = doubling_all_gather(plane_rows, n_vocab)
        group = hidden.shape[0] // n_vocab
        beam_columns = (
            gathered.reshape(n_vocab, n_dp, group, columns_here)
            .transpose(1, 0, 2, 3)
            .reshape(n_dp * n_vocab * group, columns_here)
        )

    with jax.named_scope("dense_logits"):
        full = jnp.einsum(
            "bd,vd->bv", beam_columns, out_weight, preferred_element_type=jnp.float32
        )
        full4 = full.reshape(n_blk, BB, n_tb, TB)
        rows = jnp.arange(n_blk, dtype=jnp.int32)[:, None]
        picked = full4[rows, :, block_lists, :]

    logits = lax.psum_scatter(picked, "dp", scatter_dimension=0, tiled=True)

    with jax.named_scope("softmax_stats"):
        live = jnp.arange(MOST, dtype=jnp.int32)[None, :] < own_counts[:, None]
        live_mask = live[:, :, None, None]
        masked = jnp.where(live_mask, logits, -jnp.inf)
        local_max = jnp.max(masked, axis=(1, 3))
        local_total = jnp.sum(jnp.exp(masked - local_max[:, None, :, None]), axis=(1, 3))
        stats = lax.all_gather(jnp.stack([local_max, local_total]), "vocab", axis=0)
        beam_max = jnp.max(stats[:, 0], axis=0)
        beam_total = jnp.sum(stats[:, 1] * jnp.exp(stats[:, 0] - beam_max[None]), axis=0)
        shifted = logits - beam_max[:, None, :, None] - jnp.log(beam_total)[:, None, :, None]
        allowed_logprob = jnp.where(live_mask, shifted, 0.0)
        probabilities = jnp.where(live_mask, jnp.exp(shifted), 0.0).astype(jnp.bfloat16)

    prob_part = lax.all_gather(probabilities, "dp", axis=0, tiled=True)

    rows_per_dev = n_blk * BB // n_vocab
    pairs = BB // rows_per_dev // 2
    onehot = (
        block_lists[:, :, None] == jnp.arange(n_tb, dtype=jnp.int32)[None, None, :]
    ).astype(jnp.bfloat16)
    halves = prob_part.reshape(n_blk, MOST, pairs, 2, rows_per_dev, TB)
    low_bit = lax.axis_index("vocab") % 2

    def expected_half(which):
        with jax.named_scope("dense_expected"):
            chosen = lax.dynamic_index_in_dim(halves, which, axis=3, keepdims=False)
            chosen = chosen.reshape(n_blk, MOST, pairs * rows_per_dev, TB)
            spread = jnp.einsum(
                "bsk,bsrt->brkt", onehot, chosen, preferred_element_type=jnp.float32
            ).astype(jnp.bfloat16)
            term = jnp.einsum(
                "brkt,ktd->brd",
                spread,
                out_weight.reshape(n_tb, TB, columns_here),
                preferred_element_type=jnp.float32,
            )
            return term.reshape(n_blk * pairs, rows_per_dev, columns_here)

    send_half = expected_half(1 - low_bit)
    send_half, halves = lax.optimization_barrier((send_half, halves))
    keep_half = lax.optimization_barrier(expected_half(low_bit))
    summed = halving_reduce_scatter(keep_half, send_half, n_vocab)
    squares = butterfly_sum(jnp.sum(summed * summed, axis=1), "dp", n_dp)
    width = hidden.shape[1] * n_vocab
    expected = summed * lax.rsqrt(squares / width + 1e-06)[:, None]
    return (allowed_logprob[None], expected)


def solution(mesh):
    in_specs = (P("dp", "vocab"), P("vocab", "dp"), P("vocab", None, None), P("vocab", None))
    out_specs = (P("vocab", "dp", None, None, None), P("vocab", "dp"))
    return jax.shard_map(
        per_device, mesh=mesh, in_specs=in_specs, out_specs=out_specs, check_vma=False
    )
```

```python
import jax
import jax.numpy as jnp
from jax import lax
from jax.sharding import PartitionSpec as P

TB = 128
BB = 128
MOST = 16


def exchange_stage(x, remaining, bit, n):
    me = lax.axis_index("vocab")
    axis = remaining.index(bit)
    mine = (me // (1 << bit)) % 2
    keep = lax.dynamic_index_in_dim(x, mine, axis=axis, keepdims=False)
    send = lax.dynamic_index_in_dim(x, 1 - mine, axis=axis, keepdims=False)
    perm = [(s, s ^ (1 << bit)) for s in range(n)]
    got = lax.ppermute(send, "vocab", perm=perm)
    return keep + got, [b for b in remaining if b != bit]


def halving_reduce_scatter(keep, send, n):
    levels = n.bit_length() - 1
    _, group, cols = keep.shape
    perm = [(s, s ^ 1) for s in range(n)]
    with jax.named_scope("summed_core_stage"):
        x = keep + lax.ppermute(send, "vocab", perm=perm)
    x = x.reshape([2] * (levels - 1) + [group, cols])
    remaining = list(range(levels - 1, 0, -1))
    half = cols // 2
    first, second = x[..., :half], x[..., half:]
    rest_a, rest_b = list(remaining), list(remaining)
    order_a = sorted(remaining)
    order_b = sorted(remaining, reverse=True)
    for step in range(len(order_a)):
        with jax.named_scope("summed_chip_stage"):
            first, rest_a = exchange_stage(first, rest_a, order_a[step], n)
            second, rest_b = exchange_stage(second, rest_b, order_b[step], n)
    return jnp.concatenate([first, second], axis=-1)


def gather_stage(x, have, bit, n):
    me = lax.axis_index("vocab")
    mine = (me // (1 << bit)) % 2
    perm = [(s, s ^ (1 << bit)) for s in range(n)]
    got = lax.ppermute(x, "vocab", perm=perm)
    pos = len([b for b in have if b > bit])
    low = jnp.stack([x, got], axis=pos)
    high = jnp.stack([got, x], axis=pos)
    return jnp.where(mine == 0, low, high), sorted(have + [bit], reverse=True)


def doubling_all_gather(x, n):
    levels = n.bit_length() - 1
    rows, cols = x.shape
    half = cols // 2
    first, second = x[:, :half], x[:, half:]
    have_a, have_b = [], []
    order_a = list(range(1, levels)) + [0]
    order_b = list(range(levels - 1, 0, -1)) + [0]
    for step in range(levels):
        with jax.named_scope("hidden_gather_stage"):
            first, have_a = gather_stage(first, have_a, order_a[step], n)
            second, have_b = gather_stage(second, have_b, order_b[step], n)
    joined = jnp.concatenate([first, second], axis=-1)
    return joined.reshape(n * rows, cols)


def butterfly_sum(x, axis_name, n):
    levels = n.bit_length() - 1
    for bit in range(levels):
        perm = [(s, s ^ (1 << bit)) for s in range(n)]
        x = x + lax.ppermute(x, axis_name, perm=perm)
    return x


def bruck_all_to_all(x, axis_name, n, split_axis, concat_axis):
    me = lax.axis_index(axis_name)
    levels = n.bit_length() - 1
    shape = list(x.shape)
    shape[split_axis : split_axis + 1] = [n, x.shape[split_axis] // n]
    pieces = jnp.moveaxis(x.reshape(shape), split_axis, 0)
    rest = pieces.shape[1:]
    held = pieces.reshape([2] * levels + list(rest))
    for bit in range(levels):
        pos = levels - 1 - bit
        mine = (me // (1 << bit)) % 2
        keep = lax.dynamic_index_in_dim(held, mine, axis=pos, keepdims=False)
        send = lax.dynamic_index_in_dim(held, 1 - mine, axis=pos, keepdims=False)
        perm = [(s, s ^ (1 << bit)) for s in range(n)]
        got = lax.ppermute(send, axis_name, perm=perm)
        low = jnp.stack([keep, got], axis=pos)
        high = jnp.stack([got, keep], axis=pos)
        held = jnp.where(mine == 0, low, high)
    by_source = held.reshape((n,) + tuple(rest))
    return jnp.concatenate([by_source[k] for k in range(n)], axis=concat_axis)


def direct_spread(hidden, n_vocab, n_dp):
    rows, chunk = hidden.shape
    per_slice = n_vocab // n_dp
    group = rows // n_vocab
    me_v = lax.axis_index("vocab")
    me_d = lax.axis_index("dp")
    pieces = hidden.reshape(n_vocab, group, chunk)
    got = []
    for shift in range(n_vocab):
        target = (me_v % per_slice + per_slice * me_d + shift) % n_vocab
        send = lax.dynamic_index_in_dim(pieces, target, axis=0, keepdims=False)
        perm = []
        for d in range(n_dp):
            for v in range(n_vocab):
                k = (v % per_slice + per_slice * d + shift) % n_vocab
                perm.append((d * n_vocab + v, (v // per_slice) * n_vocab + k))
        got.append(lax.ppermute(send, ("dp", "vocab"), perm=perm))
    received = jnp.stack(got)
    slot = jnp.arange(n_vocab, dtype=jnp.int32)
    order = (me_v - slot) % n_vocab
    placed = jnp.take(received, order, axis=0)
    placed = placed.reshape(n_dp, per_slice, group, chunk).transpose(0, 2, 1, 3)
    return placed.reshape(n_dp * group, per_slice * chunk)


def per_device(hidden, out_weight, token_blocks, counts):
    vocab_here, columns_here = out_weight.shape
    n_vocab = lax.psum(1, "vocab")
    n_dp = lax.psum(1, "dp")
    n_tb = vocab_here // TB
    block_lists = token_blocks[0]
    block_counts = counts[0]
    n_blk = block_lists.shape[0]
    own_blocks = hidden.shape[0] // BB
    assert own_blocks == 1 and n_blk == n_dp
    me_dp = lax.axis_index("dp")
    own_counts = lax.dynamic_slice_in_dim(block_counts, me_dp, 1, 0)

    with jax.named_scope("hidden_spread"):
        plane_rows = direct_spread(hidden, n_vocab, n_dp)
        gathered = doubling_all_gather(plane_rows, n_vocab)
        group = hidden.shape[0] // n_vocab
        beam_columns = (
            gathered.reshape(n_vocab, n_dp, group, columns_here)
            .transpose(1, 0, 2, 3)
            .reshape(n_dp * n_vocab * group, columns_here)
        )

    with jax.named_scope("dense_logits"):
        full = jnp.einsum(
            "bd,vd->bv", beam_columns, out_weight, preferred_element_type=jnp.float32
        )
        full4 = full.reshape(n_blk, BB, n_tb, TB)
        pick = (
            block_lists[:, :, None] == jnp.arange(n_tb, dtype=jnp.int32)[None, None, :]
        ).astype(jnp.float32)
        picked = jnp.einsum(
            "bsk,brkt->bsrt", pick, full4, precision=lax.Precision.HIGHEST,
            preferred_element_type=jnp.float32,
        )

    logits = lax.psum_scatter(picked, "dp", scatter_dimension=0, tiled=True)

    with jax.named_scope("softmax_stats"):
        live = jnp.arange(MOST, dtype=jnp.int32)[None, :] < own_counts[:, None]
        live_mask = live[:, :, None, None]
        masked = jnp.where(live_mask, logits, -jnp.inf)
        local_max = jnp.max(masked, axis=(1, 3))
        local_total = jnp.sum(jnp.exp(masked - local_max[:, None, :, None]), axis=(1, 3))
        stats = lax.all_gather(jnp.stack([local_max, local_total]), "vocab", axis=0)
        beam_max = jnp.max(stats[:, 0], axis=0)
        beam_total = jnp.sum(stats[:, 1] * jnp.exp(stats[:, 0] - beam_max[None]), axis=0)
        shifted = logits - beam_max[:, None, :, None] - jnp.log(beam_total)[:, None, :, None]
        allowed_logprob = jnp.where(live_mask, shifted, 0.0)
        probabilities = jnp.where(live_mask, jnp.exp(shifted), 0.0).astype(jnp.bfloat16)

    prob_part = lax.all_gather(probabilities, "dp", axis=0, tiled=True)

    rows_per_dev = n_blk * BB // n_vocab
    pairs = BB // rows_per_dev // 2
    onehot = (
        block_lists[:, :, None] == jnp.arange(n_tb, dtype=jnp.int32)[None, None, :]
    ).astype(jnp.bfloat16)
    halves = prob_part.reshape(n_blk, MOST, pairs, 2, rows_per_dev, TB)
    low_bit = lax.axis_index("vocab") % 2

    def expected_half(which):
        with jax.named_scope("dense_expected"):
            chosen = lax.dynamic_index_in_dim(halves, which, axis=3, keepdims=False)
            chosen = chosen.reshape(n_blk, MOST, pairs * rows_per_dev, TB)
            spread = jnp.einsum(
                "bsk,bsrt->brkt", onehot, chosen, preferred_element_type=jnp.float32
            ).astype(jnp.bfloat16)
            term = jnp.einsum(
                "brkt,ktd->brd",
                spread,
                out_weight.reshape(n_tb, TB, columns_here),
                preferred_element_type=jnp.float32,
            )
            return term.reshape(n_blk * pairs, rows_per_dev, columns_here)

    send_half = expected_half(1 - low_bit)
    keep_half = expected_half(low_bit)
    summed = halving_reduce_scatter(keep_half, send_half, n_vocab)
    squares = butterfly_sum(jnp.sum(summed * summed, axis=1), "dp", n_dp)
    width = hidden.shape[1] * n_vocab
    expected = summed * lax.rsqrt(squares / width + 1e-06)[:, None]
    return (allowed_logprob[None], expected)


def solution(mesh):
    in_specs = (P("dp", "vocab"), P("vocab", "dp"), P("vocab", None, None), P("vocab", None))
    out_specs = (P("vocab", "dp", None, None, None), P("vocab", "dp"))
    return jax.shard_map(
        per_device, mesh=mesh, in_specs=in_specs, out_specs=out_specs, check_vma=False
    )
```

```python
import jax
import jax.numpy as jnp
from jax import lax
from jax.sharding import PartitionSpec as P

TB = 128
BB = 128
MOST = 16


def exchange_stage(x, remaining, bit, n):
    me = lax.axis_index("vocab")
    axis = remaining.index(bit)
    mine = (me // (1 << bit)) % 2
    keep = lax.dynamic_index_in_dim(x, mine, axis=axis, keepdims=False)
    send = lax.dynamic_index_in_dim(x, 1 - mine, axis=axis, keepdims=False)
    perm = [(s, s ^ (1 << bit)) for s in range(n)]
    got = lax.ppermute(send, "vocab", perm=perm)
    return keep + got, [b for b in remaining if b != bit]


def halving_reduce_scatter(keep, send, n):
    levels = n.bit_length() - 1
    _, group, cols = keep.shape
    perm = [(s, s ^ 1) for s in range(n)]
    with jax.named_scope("summed_core_stage"):
        x = keep + lax.ppermute(send, "vocab", perm=perm)
    x = x.reshape([2] * (levels - 1) + [group, cols])
    remaining = list(range(levels - 1, 0, -1))
    half = cols // 2
    first, second = x[..., :half], x[..., half:]
    rest_a, rest_b = list(remaining), list(remaining)
    order_a = sorted(remaining)
    order_b = sorted(remaining, reverse=True)
    for step in range(len(order_a)):
        with jax.named_scope("summed_chip_stage"):
            first, rest_a = exchange_stage(first, rest_a, order_a[step], n)
            second, rest_b = exchange_stage(second, rest_b, order_b[step], n)
    return jnp.concatenate([first, second], axis=-1)


def gather_stage(x, have, bit, n):
    me = lax.axis_index("vocab")
    mine = (me // (1 << bit)) % 2
    perm = [(s, s ^ (1 << bit)) for s in range(n)]
    got = lax.ppermute(x, "vocab", perm=perm)
    pos = len([b for b in have if b > bit])
    low = jnp.stack([x, got], axis=pos)
    high = jnp.stack([got, x], axis=pos)
    return jnp.where(mine == 0, low, high), sorted(have + [bit], reverse=True)


def doubling_all_gather(x, n):
    levels = n.bit_length() - 1
    rows, cols = x.shape
    half = cols // 2
    first, second = x[:, :half], x[:, half:]
    have_a, have_b = [], []
    order_a = list(range(1, levels)) + [0]
    order_b = list(range(levels - 1, 0, -1)) + [0]
    for step in range(levels):
        with jax.named_scope("hidden_gather_stage"):
            first, have_a = gather_stage(first, have_a, order_a[step], n)
            second, have_b = gather_stage(second, have_b, order_b[step], n)
    joined = jnp.concatenate([first, second], axis=-1)
    return joined.reshape(n * rows, cols)


def butterfly_sum(x, axis_name, n):
    levels = n.bit_length() - 1
    for bit in range(levels):
        perm = [(s, s ^ (1 << bit)) for s in range(n)]
        x = x + lax.ppermute(x, axis_name, perm=perm)
    return x


def bruck_all_to_all(x, axis_name, n, split_axis, concat_axis):
    me = lax.axis_index(axis_name)
    levels = n.bit_length() - 1
    shape = list(x.shape)
    shape[split_axis : split_axis + 1] = [n, x.shape[split_axis] // n]
    pieces = jnp.moveaxis(x.reshape(shape), split_axis, 0)
    rest = pieces.shape[1:]
    held = pieces.reshape([2] * levels + list(rest))
    for bit in range(levels):
        pos = levels - 1 - bit
        mine = (me // (1 << bit)) % 2
        keep = lax.dynamic_index_in_dim(held, mine, axis=pos, keepdims=False)
        send = lax.dynamic_index_in_dim(held, 1 - mine, axis=pos, keepdims=False)
        perm = [(s, s ^ (1 << bit)) for s in range(n)]
        got = lax.ppermute(send, axis_name, perm=perm)
        low = jnp.stack([keep, got], axis=pos)
        high = jnp.stack([got, keep], axis=pos)
        held = jnp.where(mine == 0, low, high)
    by_source = held.reshape((n,) + tuple(rest))
    return jnp.concatenate([by_source[k] for k in range(n)], axis=concat_axis)


def line_all_gather(own_part, n):
    me = lax.axis_index("dp")
    got = [own_part]
    from_left, from_right = own_part, own_part
    for step in range(1, n):
        upward = [(s, s + 1) for s in range(step - 1, n - 1)]
        downward = [(s, s - 1) for s in range(1, n - step + 1)]
        from_left, from_right = lax.optimization_barrier((from_left, from_right))
        from_left = lax.ppermute(from_left, "dp", perm=upward)
        from_right = lax.ppermute(from_right, "dp", perm=downward)
        got += [from_left, from_right]
    blocks = []
    for block in range(n):
        pick = jnp.where(me == block, got[0], jnp.zeros_like(got[0]))
        for step in range(1, n):
            pick = jnp.where(me - step == block, got[2 * step - 1], pick)
            pick = jnp.where(me + step == block, got[2 * step], pick)
        blocks.append(pick)
    return jnp.stack(blocks)


def per_device(hidden, out_weight, token_blocks, counts):
    vocab_here, columns_here = out_weight.shape
    n_vocab = lax.psum(1, "vocab")
    n_dp = lax.psum(1, "dp")
    n_tb = vocab_here // TB
    block_lists = token_blocks[0]
    block_counts = counts[0]
    n_blk = block_lists.shape[0]
    own_blocks = hidden.shape[0] // BB
    assert own_blocks == 1 and n_blk == n_dp
    me_dp = lax.axis_index("dp")
    own_counts = lax.dynamic_slice_in_dim(block_counts, me_dp, 1, 0)

    with jax.named_scope("hidden_spread"):
        row_slices = bruck_all_to_all(hidden, "vocab", n_vocab, split_axis=0, concat_axis=1)
        plane_rows = bruck_all_to_all(row_slices, "dp", n_dp, split_axis=1, concat_axis=0)
        gathered = doubling_all_gather(plane_rows, n_vocab)
        group = hidden.shape[0] // n_vocab
        beam_columns = (
            gathered.reshape(n_vocab, n_dp, group, columns_here)
            .transpose(1, 0, 2, 3)
            .reshape(n_dp * n_vocab * group, columns_here)
        )

    with jax.named_scope("dense_logits"):
        full = jnp.einsum(
            "bd,vd->bv", beam_columns, out_weight, preferred_element_type=jnp.float32
        )
        full4 = full.reshape(n_blk, BB, n_tb, TB)
        rows = jnp.arange(n_blk, dtype=jnp.int32)[:, None]
        picked = full4[rows, :, block_lists, :]

    logits = lax.psum_scatter(picked, "dp", scatter_dimension=0, tiled=True)

    with jax.named_scope("softmax_stats"):
        live = jnp.arange(MOST, dtype=jnp.int32)[None, :] < own_counts[:, None]
        live_mask = live[:, :, None, None]
        masked = jnp.where(live_mask, logits, -jnp.inf)
        local_max = jnp.max(masked, axis=(1, 3))
        local_total = jnp.sum(jnp.exp(masked - local_max[:, None, :, None]), axis=(1, 3))
        stats = lax.all_gather(jnp.stack([local_max, local_total]), "vocab", axis=0)
        beam_max = jnp.max(stats[:, 0], axis=0)
        beam_total = jnp.sum(stats[:, 1] * jnp.exp(stats[:, 0] - beam_max[None]), axis=0)
        shifted = logits - beam_max[:, None, :, None] - jnp.log(beam_total)[:, None, :, None]
        allowed_logprob = jnp.where(live_mask, shifted, 0.0)
        probabilities = jnp.where(live_mask, jnp.exp(shifted), 0.0).astype(jnp.bfloat16)

    with jax.named_scope("probs_two_routes"):
        first_rows = probabilities[:, :, : BB // 2]
        second_rows = probabilities[0, :, BB // 2 :]
        by_queue = lax.all_gather(first_rows, "dp", axis=0, tiled=True)
        by_permute = line_all_gather(second_rows, n_dp)
        prob_part = jnp.concatenate([by_queue, by_permute], axis=2)

    rows_per_dev = n_blk * BB // n_vocab
    pairs = BB // rows_per_dev // 2
    onehot = (
        block_lists[:, :, None] == jnp.arange(n_tb, dtype=jnp.int32)[None, None, :]
    ).astype(jnp.bfloat16)
    halves = prob_part.reshape(n_blk, MOST, pairs, 2, rows_per_dev, TB)
    low_bit = lax.axis_index("vocab") % 2

    def expected_half(which):
        with jax.named_scope("dense_expected"):
            chosen = lax.dynamic_index_in_dim(halves, which, axis=3, keepdims=False)
            chosen = chosen.reshape(n_blk, MOST, pairs * rows_per_dev, TB)
            spread = jnp.einsum(
                "bsk,bsrt->brkt", onehot, chosen, preferred_element_type=jnp.float32
            ).astype(jnp.bfloat16)
            term = jnp.einsum(
                "brkt,ktd->brd",
                spread,
                out_weight.reshape(n_tb, TB, columns_here),
                preferred_element_type=jnp.float32,
            )
            return term.reshape(n_blk * pairs, rows_per_dev, columns_here)

    send_half = expected_half(1 - low_bit)
    keep_half = expected_half(low_bit)
    summed = halving_reduce_scatter(keep_half, send_half, n_vocab)
    squares = butterfly_sum(jnp.sum(summed * summed, axis=1), "dp", n_dp)
    width = hidden.shape[1] * n_vocab
    expected = summed * lax.rsqrt(squares / width + 1e-06)[:, None]
    return (allowed_logprob[None], expected)


def solution(mesh):
    in_specs = (P("dp", "vocab"), P("vocab", "dp"), P("vocab", None, None), P("vocab", None))
    out_specs = (P("vocab", "dp", None, None, None), P("vocab", "dp"))
    return jax.shard_map(
        per_device, mesh=mesh, in_specs=in_specs, out_specs=out_specs, check_vma=False
    )
```

```python
import jax
import jax.numpy as jnp
from jax import lax
from jax.sharding import PartitionSpec as P

TB = 128
BB = 128
MOST = 16


def exchange_stage(x, remaining, bit, n):
    me = lax.axis_index("vocab")
    axis = remaining.index(bit)
    mine = (me // (1 << bit)) % 2
    keep = lax.dynamic_index_in_dim(x, mine, axis=axis, keepdims=False)
    send = lax.dynamic_index_in_dim(x, 1 - mine, axis=axis, keepdims=False)
    perm = [(s, s ^ (1 << bit)) for s in range(n)]
    got = lax.ppermute(send, "vocab", perm=perm)
    return keep + got, [b for b in remaining if b != bit]


def halving_reduce_scatter(keep, send, n):
    levels = n.bit_length() - 1
    _, group, cols = keep.shape
    perm = [(s, s ^ 1) for s in range(n)]
    with jax.named_scope("summed_core_stage"):
        x = keep + lax.ppermute(send, "vocab", perm=perm)
    x = x.reshape([2] * (levels - 1) + [group, cols])
    remaining = list(range(levels - 1, 0, -1))
    half = cols // 2
    first, second = x[..., :half], x[..., half:]
    rest_a, rest_b = list(remaining), list(remaining)
    order_a = sorted(remaining)
    order_b = sorted(remaining, reverse=True)
    for step in range(len(order_a)):
        with jax.named_scope("summed_chip_stage"):
            first, rest_a = exchange_stage(first, rest_a, order_a[step], n)
            second, rest_b = exchange_stage(second, rest_b, order_b[step], n)
    return jnp.concatenate([first, second], axis=-1)


def gather_stage(x, have, bit, n):
    me = lax.axis_index("vocab")
    mine = (me // (1 << bit)) % 2
    perm = [(s, s ^ (1 << bit)) for s in range(n)]
    got = lax.ppermute(x, "vocab", perm=perm)
    pos = len([b for b in have if b > bit])
    low = jnp.stack([x, got], axis=pos)
    high = jnp.stack([got, x], axis=pos)
    return jnp.where(mine == 0, low, high), sorted(have + [bit], reverse=True)


def doubling_all_gather(x, n):
    levels = n.bit_length() - 1
    rows, cols = x.shape
    half = cols // 2
    quarter = cols // 4
    offloaded = lax.all_gather(x[:, :half], "vocab", axis=0, tiled=True)
    first, second = x[:, half : half + quarter], x[:, half + quarter :]
    have_a, have_b = [], []
    order_a = list(range(1, levels)) + [0]
    order_b = list(range(levels - 1, 0, -1)) + [0]
    for step in range(levels):
        with jax.named_scope("hidden_gather_stage"):
            first, have_a = gather_stage(first, have_a, order_a[step], n)
            second, have_b = gather_stage(second, have_b, order_b[step], n)
    joined = jnp.concatenate([first, second], axis=-1).reshape(n * rows, cols - half)
    return jnp.concatenate([offloaded, joined], axis=-1)


def butterfly_sum(x, axis_name, n):
    levels = n.bit_length() - 1
    for bit in range(levels):
        perm = [(s, s ^ (1 << bit)) for s in range(n)]
        x = x + lax.ppermute(x, axis_name, perm=perm)
    return x


def bruck_all_to_all(x, axis_name, n, split_axis, concat_axis):
    me = lax.axis_index(axis_name)
    levels = n.bit_length() - 1
    shape = list(x.shape)
    shape[split_axis : split_axis + 1] = [n, x.shape[split_axis] // n]
    pieces = jnp.moveaxis(x.reshape(shape), split_axis, 0)
    rest = pieces.shape[1:]
    held = pieces.reshape([2] * levels + list(rest))
    for bit in range(levels):
        pos = levels - 1 - bit
        mine = (me // (1 << bit)) % 2
        keep = lax.dynamic_index_in_dim(held, mine, axis=pos, keepdims=False)
        send = lax.dynamic_index_in_dim(held, 1 - mine, axis=pos, keepdims=False)
        perm = [(s, s ^ (1 << bit)) for s in range(n)]
        got = lax.ppermute(send, axis_name, perm=perm)
        low = jnp.stack([keep, got], axis=pos)
        high = jnp.stack([got, keep], axis=pos)
        held = jnp.where(mine == 0, low, high)
    by_source = held.reshape((n,) + tuple(rest))
    return jnp.concatenate([by_source[k] for k in range(n)], axis=concat_axis)


def per_device(hidden, out_weight, token_blocks, counts):
    vocab_here, columns_here = out_weight.shape
    n_vocab = lax.psum(1, "vocab")
    n_dp = lax.psum(1, "dp")
    n_tb = vocab_here // TB
    block_lists = token_blocks[0]
    block_counts = counts[0]
    n_blk = block_lists.shape[0]
    own_blocks = hidden.shape[0] // BB
    assert own_blocks == 1 and n_blk == n_dp
    me_dp = lax.axis_index("dp")
    own_counts = lax.dynamic_slice_in_dim(block_counts, me_dp, 1, 0)

    with jax.named_scope("hidden_spread"):
        row_slices = bruck_all_to_all(hidden, "vocab", n_vocab, split_axis=0, concat_axis=1)
        plane_rows = bruck_all_to_all(row_slices, "dp", n_dp, split_axis=1, concat_axis=0)
        gathered = doubling_all_gather(plane_rows, n_vocab)
        group = hidden.shape[0] // n_vocab
        beam_columns = (
            gathered.reshape(n_vocab, n_dp, group, columns_here)
            .transpose(1, 0, 2, 3)
            .reshape(n_dp * n_vocab * group, columns_here)
        )

    with jax.named_scope("dense_logits"):
        full = jnp.einsum(
            "bd,vd->bv", beam_columns, out_weight, preferred_element_type=jnp.float32
        )
        full4 = full.reshape(n_blk, BB, n_tb, TB)
        rows = jnp.arange(n_blk, dtype=jnp.int32)[:, None]
        picked = full4[rows, :, block_lists, :]

    logits = lax.psum_scatter(picked, "dp", scatter_dimension=0, tiled=True)

    with jax.named_scope("softmax_stats"):
        live = jnp.arange(MOST, dtype=jnp.int32)[None, :] < own_counts[:, None]
        live_mask = live[:, :, None, None]
        masked = jnp.where(live_mask, logits, -jnp.inf)
        local_max = jnp.max(masked, axis=(1, 3))
        local_total = jnp.sum(jnp.exp(masked - local_max[:, None, :, None]), axis=(1, 3))
        stats = lax.all_gather(jnp.stack([local_max, local_total]), "vocab", axis=0)
        beam_max = jnp.max(stats[:, 0], axis=0)
        beam_total = jnp.sum(stats[:, 1] * jnp.exp(stats[:, 0] - beam_max[None]), axis=0)
        shifted = logits - beam_max[:, None, :, None] - jnp.log(beam_total)[:, None, :, None]
        allowed_logprob = jnp.where(live_mask, shifted, 0.0)
        probabilities = jnp.where(live_mask, jnp.exp(shifted), 0.0).astype(jnp.bfloat16)

    prob_part = lax.all_gather(probabilities, "dp", axis=0, tiled=True)

    rows_per_dev = n_blk * BB // n_vocab
    pairs = BB // rows_per_dev // 2
    onehot = (
        block_lists[:, :, None] == jnp.arange(n_tb, dtype=jnp.int32)[None, None, :]
    ).astype(jnp.bfloat16)
    halves = prob_part.reshape(n_blk, MOST, pairs, 2, rows_per_dev, TB)
    low_bit = lax.axis_index("vocab") % 2

    def expected_half(which):
        with jax.named_scope("dense_expected"):
            chosen = lax.dynamic_index_in_dim(halves, which, axis=3, keepdims=False)
            chosen = chosen.reshape(n_blk, MOST, pairs * rows_per_dev, TB)
            spread = jnp.einsum(
                "bsk,bsrt->brkt", onehot, chosen, preferred_element_type=jnp.float32
            ).astype(jnp.bfloat16)
            term = jnp.einsum(
                "brkt,ktd->brd",
                spread,
                out_weight.reshape(n_tb, TB, columns_here),
                preferred_element_type=jnp.float32,
            )
            return term.reshape(n_blk * pairs, rows_per_dev, columns_here)

    send_half = expected_half(1 - low_bit)
    keep_half = expected_half(low_bit)
    summed = halving_reduce_scatter(keep_half, send_half, n_vocab)
    squares = butterfly_sum(jnp.sum(summed * summed, axis=1), "dp", n_dp)
    width = hidden.shape[1] * n_vocab
    expected = summed * lax.rsqrt(squares / width + 1e-06)[:, None]
    return (allowed_logprob[None], expected)


def solution(mesh):
    in_specs = (P("dp", "vocab"), P("vocab", "dp"), P("vocab", None, None), P("vocab", None))
    out_specs = (P("vocab", "dp", None, None, None), P("vocab", "dp"))
    return jax.shard_map(
        per_device, mesh=mesh, in_specs=in_specs, out_specs=out_specs, check_vma=False
    )
```

```python
import jax
import jax.numpy as jnp
from jax import lax
from jax.sharding import PartitionSpec as P

TB = 128
BB = 128
MOST = 16


def exchange_stage(x, remaining, bit, n):
    me = lax.axis_index("vocab")
    axis = remaining.index(bit)
    mine = (me // (1 << bit)) % 2
    keep = lax.dynamic_index_in_dim(x, mine, axis=axis, keepdims=False)
    send = lax.dynamic_index_in_dim(x, 1 - mine, axis=axis, keepdims=False)
    perm = [(s, s ^ (1 << bit)) for s in range(n)]
    got = lax.ppermute(send, "vocab", perm=perm)
    return keep + got, [b for b in remaining if b != bit]


def halving_reduce_scatter(keep, send, n):
    levels = n.bit_length() - 1
    _, group, cols = keep.shape
    perm = [(s, s ^ 1) for s in range(n)]
    with jax.named_scope("summed_core_stage"):
        x = keep + lax.ppermute(send, "vocab", perm=perm)
    x = x.reshape([2] * (levels - 1) + [group, cols])
    remaining = list(range(levels - 1, 0, -1))
    half = cols // 2
    first, second = x[..., :half], x[..., half:]
    rest_a, rest_b = list(remaining), list(remaining)
    order_a = sorted(remaining)
    order_b = sorted(remaining, reverse=True)
    for step in range(len(order_a)):
        with jax.named_scope("summed_chip_stage"):
            first, rest_a = exchange_stage(first, rest_a, order_a[step], n)
            second, rest_b = exchange_stage(second, rest_b, order_b[step], n)
    return jnp.concatenate([first, second], axis=-1)


def gather_stage(x, have, bit, n):
    me = lax.axis_index("vocab")
    mine = (me // (1 << bit)) % 2
    perm = [(s, s ^ (1 << bit)) for s in range(n)]
    got = lax.ppermute(x, "vocab", perm=perm)
    pos = len([b for b in have if b > bit])
    low = jnp.stack([x, got], axis=pos)
    high = jnp.stack([got, x], axis=pos)
    return jnp.where(mine == 0, low, high), sorted(have + [bit], reverse=True)


def doubling_all_gather(x, n):
    levels = n.bit_length() - 1
    rows, cols = x.shape
    half = cols // 2
    first, second = x[:, :half], x[:, half:]
    have_a, have_b = [], []
    order_a = list(range(1, levels)) + [0]
    order_b = list(range(levels - 1, 0, -1)) + [0]
    for step in range(levels):
        with jax.named_scope("hidden_gather_stage"):
            first, have_a = gather_stage(first, have_a, order_a[step], n)
            second, have_b = gather_stage(second, have_b, order_b[step], n)
    joined = jnp.concatenate([first, second], axis=-1)
    return joined.reshape(n * rows, cols)


def butterfly_sum(x, axis_name, n):
    levels = n.bit_length() - 1
    for bit in range(levels):
        perm = [(s, s ^ (1 << bit)) for s in range(n)]
        x = x + lax.ppermute(x, axis_name, perm=perm)
    return x


def bruck_all_to_all(x, axis_name, n, split_axis, concat_axis):
    me = lax.axis_index(axis_name)
    levels = n.bit_length() - 1
    shape = list(x.shape)
    shape[split_axis : split_axis + 1] = [n, x.shape[split_axis] // n]
    pieces = jnp.moveaxis(x.reshape(shape), split_axis, 0)
    rest = pieces.shape[1:]
    held = pieces.reshape([2] * levels + list(rest))
    for bit in range(levels):
        pos = levels - 1 - bit
        mine = (me // (1 << bit)) % 2
        keep = lax.dynamic_index_in_dim(held, mine, axis=pos, keepdims=False)
        send = lax.dynamic_index_in_dim(held, 1 - mine, axis=pos, keepdims=False)
        perm = [(s, s ^ (1 << bit)) for s in range(n)]
        got = lax.ppermute(send, axis_name, perm=perm)
        low = jnp.stack([keep, got], axis=pos)
        high = jnp.stack([got, keep], axis=pos)
        held = jnp.where(mine == 0, low, high)
    by_source = held.reshape((n,) + tuple(rest))
    return jnp.concatenate([by_source[k] for k in range(n)], axis=concat_axis)


def per_device(hidden, out_weight, token_blocks, counts):
    vocab_here, columns_here = out_weight.shape
    n_vocab = lax.psum(1, "vocab")
    n_dp = lax.psum(1, "dp")
    n_tb = vocab_here // TB
    block_lists = token_blocks[0]
    block_counts = counts[0]
    n_blk = block_lists.shape[0]
    own_blocks = hidden.shape[0] // BB
    assert own_blocks == 1 and n_blk == n_dp
    me_dp = lax.axis_index("dp")
    own_counts = lax.dynamic_slice_in_dim(block_counts, me_dp, 1, 0)

    with jax.named_scope("hidden_spread"):
        row_slices = bruck_all_to_all(hidden, "vocab", n_vocab, split_axis=0, concat_axis=1)
        plane_rows = bruck_all_to_all(row_slices, "dp", n_dp, split_axis=1, concat_axis=0)
        gathered = doubling_all_gather(plane_rows, n_vocab)
        group = hidden.shape[0] // n_vocab

    with jax.named_scope("dense_logits"):
        full = jnp.einsum(
            "bd,vd->bv", gathered, out_weight, preferred_element_type=jnp.float32
        )
        full6 = full.reshape(n_vocab, n_blk, group, n_tb, TB)
        rows = jnp.arange(n_blk, dtype=jnp.int32)[:, None]
        picked = full6[:, rows, :, block_lists, :].reshape(n_blk, MOST, BB, TB)

    logits = lax.psum_scatter(picked, "dp", scatter_dimension=0, tiled=True)

    with jax.named_scope("softmax_stats"):
        live = jnp.arange(MOST, dtype=jnp.int32)[None, :] < own_counts[:, None]
        live_mask = live[:, :, None, None]
        masked = jnp.where(live_mask, logits, -jnp.inf)
        local_max = jnp.max(masked, axis=(1, 3))
        local_total = jnp.sum(jnp.exp(masked - local_max[:, None, :, None]), axis=(1, 3))
        stats = lax.all_gather(jnp.stack([local_max, local_total]), "vocab", axis=0)
        beam_max = jnp.max(stats[:, 0], axis=0)
        beam_total = jnp.sum(stats[:, 1] * jnp.exp(stats[:, 0] - beam_max[None]), axis=0)
        shifted = logits - beam_max[:, None, :, None] - jnp.log(beam_total)[:, None, :, None]
        allowed_logprob = jnp.where(live_mask, shifted, 0.0)
        probabilities = jnp.where(live_mask, jnp.exp(shifted), 0.0).astype(jnp.bfloat16)

    prob_part = lax.all_gather(probabilities, "dp", axis=0, tiled=True)

    rows_per_dev = n_blk * BB // n_vocab
    pairs = BB // rows_per_dev // 2
    onehot = (
        block_lists[:, :, None] == jnp.arange(n_tb, dtype=jnp.int32)[None, None, :]
    ).astype(jnp.bfloat16)
    halves = prob_part.reshape(n_blk, MOST, pairs, 2, rows_per_dev, TB)
    low_bit = lax.axis_index("vocab") % 2

    def expected_half(which):
        with jax.named_scope("dense_expected"):
            chosen = lax.dynamic_index_in_dim(halves, which, axis=3, keepdims=False)
            chosen = chosen.reshape(n_blk, MOST, pairs * rows_per_dev, TB)
            spread = jnp.einsum(
                "bsk,bsrt->brkt", onehot, chosen, preferred_element_type=jnp.float32
            ).astype(jnp.bfloat16)
            term = jnp.einsum(
                "brkt,ktd->brd",
                spread,
                out_weight.reshape(n_tb, TB, columns_here),
                preferred_element_type=jnp.float32,
            )
            return term.reshape(n_blk * pairs, rows_per_dev, columns_here)

    send_half = expected_half(1 - low_bit)
    keep_half = expected_half(low_bit)
    summed = halving_reduce_scatter(keep_half, send_half, n_vocab)
    squares = butterfly_sum(jnp.sum(summed * summed, axis=1), "dp", n_dp)
    width = hidden.shape[1] * n_vocab
    expected = summed * lax.rsqrt(squares / width + 1e-06)[:, None]
    return (allowed_logprob[None], expected)


def solution(mesh):
    in_specs = (P("dp", "vocab"), P("vocab", "dp"), P("vocab", None, None), P("vocab", None))
    out_specs = (P("vocab", "dp", None, None, None), P("vocab", "dp"))
    return jax.shard_map(
        per_device, mesh=mesh, in_specs=in_specs, out_specs=out_specs, check_vma=False
    )
```

```python
import jax
import jax.numpy as jnp
from jax import lax
from jax.sharding import PartitionSpec as P

TB = 128
BB = 128
MOST = 16


def exchange_stage(x, remaining, bit, n):
    me = lax.axis_index("vocab")
    axis = remaining.index(bit)
    mine = (me // (1 << bit)) % 2
    keep = lax.dynamic_index_in_dim(x, mine, axis=axis, keepdims=False)
    send = lax.dynamic_index_in_dim(x, 1 - mine, axis=axis, keepdims=False)
    perm = [(s, s ^ (1 << bit)) for s in range(n)]
    got = lax.ppermute(send, "vocab", perm=perm)
    return keep + got, [b for b in remaining if b != bit]


def halving_reduce_scatter(keep, send, n):
    levels = n.bit_length() - 1
    _, group, cols = keep.shape
    perm = [(s, s ^ 1) for s in range(n)]
    half = cols // 2
    streams = []
    for cut in (slice(0, half), slice(half, cols)):
        with jax.named_scope("summed_core_stage"):
            x = keep[:, :, cut] + lax.ppermute(send[:, :, cut], "vocab", perm=perm)
        streams.append(x.reshape([2] * (levels - 1) + [group, half]))
    first, second = streams
    remaining = list(range(levels - 1, 0, -1))
    rest_a, rest_b = list(remaining), list(remaining)
    order_a = sorted(remaining)
    order_b = sorted(remaining, reverse=True)
    for step in range(len(order_a)):
        with jax.named_scope("summed_chip_stage"):
            first, rest_a = exchange_stage(first, rest_a, order_a[step], n)
            second, rest_b = exchange_stage(second, rest_b, order_b[step], n)
    return jnp.concatenate([first, second], axis=-1)


def gather_stage(x, have, bit, n):
    me = lax.axis_index("vocab")
    mine = (me // (1 << bit)) % 2
    perm = [(s, s ^ (1 << bit)) for s in range(n)]
    got = lax.ppermute(x, "vocab", perm=perm)
    pos = len([b for b in have if b > bit])
    low = jnp.stack([x, got], axis=pos)
    high = jnp.stack([got, x], axis=pos)
    return jnp.where(mine == 0, low, high), sorted(have + [bit], reverse=True)


def doubling_all_gather(x, n):
    levels = n.bit_length() - 1
    rows, cols = x.shape
    half = cols // 2
    first, second = x[:, :half], x[:, half:]
    have_a, have_b = [], []
    order_a = list(range(1, levels)) + [0]
    order_b = list(range(levels - 1, 0, -1)) + [0]
    for step in range(levels):
        with jax.named_scope("hidden_gather_stage"):
            first, have_a = gather_stage(first, have_a, order_a[step], n)
            second, have_b = gather_stage(second, have_b, order_b[step], n)
    joined = jnp.concatenate([first, second], axis=-1)
    return joined.reshape(n * rows, cols)


def butterfly_sum(x, axis_name, n):
    levels = n.bit_length() - 1
    for bit in range(levels):
        perm = [(s, s ^ (1 << bit)) for s in range(n)]
        x = x + lax.ppermute(x, axis_name, perm=perm)
    return x


def bruck_all_to_all(x, axis_name, n, split_axis, concat_axis):
    me = lax.axis_index(axis_name)
    levels = n.bit_length() - 1
    shape = list(x.shape)
    shape[split_axis : split_axis + 1] = [n, x.shape[split_axis] // n]
    pieces = jnp.moveaxis(x.reshape(shape), split_axis, 0)
    rest = pieces.shape[1:]
    held = pieces.reshape([2] * levels + list(rest))
    for bit in range(levels):
        pos = levels - 1 - bit
        mine = (me // (1 << bit)) % 2
        keep = lax.dynamic_index_in_dim(held, mine, axis=pos, keepdims=False)
        send = lax.dynamic_index_in_dim(held, 1 - mine, axis=pos, keepdims=False)
        perm = [(s, s ^ (1 << bit)) for s in range(n)]
        got = lax.ppermute(send, axis_name, perm=perm)
        low = jnp.stack([keep, got], axis=pos)
        high = jnp.stack([got, keep], axis=pos)
        held = jnp.where(mine == 0, low, high)
    by_source = held.reshape((n,) + tuple(rest))
    return jnp.concatenate([by_source[k] for k in range(n)], axis=concat_axis)


def per_device(hidden, out_weight, token_blocks, counts):
    vocab_here, columns_here = out_weight.shape
    n_vocab = lax.psum(1, "vocab")
    n_dp = lax.psum(1, "dp")
    n_tb = vocab_here // TB
    block_lists = token_blocks[0]
    block_counts = counts[0]
    n_blk = block_lists.shape[0]
    own_blocks = hidden.shape[0] // BB
    assert own_blocks == 1 and n_blk == n_dp
    me_dp = lax.axis_index("dp")
    own_counts = lax.dynamic_slice_in_dim(block_counts, me_dp, 1, 0)

    with jax.named_scope("hidden_spread"):
        row_slices = bruck_all_to_all(hidden, "vocab", n_vocab, split_axis=0, concat_axis=1)
        plane_rows = bruck_all_to_all(row_slices, "dp", n_dp, split_axis=1, concat_axis=0)
        gathered = doubling_all_gather(plane_rows, n_vocab)
        group = hidden.shape[0] // n_vocab
        beam_columns = (
            gathered.reshape(n_vocab, n_dp, group, columns_here)
            .transpose(1, 0, 2, 3)
            .reshape(n_dp * n_vocab * group, columns_here)
        )

    with jax.named_scope("dense_logits"):
        full = jnp.einsum(
            "bd,vd->bv", beam_columns, out_weight, preferred_element_type=jnp.float32
        )
        full4 = full.reshape(n_blk, BB, n_tb, TB)
        rows = jnp.arange(n_blk, dtype=jnp.int32)[:, None]
        picked = full4[rows, :, block_lists, :]

    logits = lax.psum_scatter(picked, "dp", scatter_dimension=0, tiled=True)

    with jax.named_scope("softmax_stats"):
        live = jnp.arange(MOST, dtype=jnp.int32)[None, :] < own_counts[:, None]
        live_mask = live[:, :, None, None]
        masked = jnp.where(live_mask, logits, -jnp.inf)
        local_max = jnp.max(masked, axis=(1, 3))
        local_total = jnp.sum(jnp.exp(masked - local_max[:, None, :, None]), axis=(1, 3))
        stats = lax.all_gather(jnp.stack([local_max, local_total]), "vocab", axis=0)
        beam_max = jnp.max(stats[:, 0], axis=0)
        beam_total = jnp.sum(stats[:, 1] * jnp.exp(stats[:, 0] - beam_max[None]), axis=0)
        shifted = logits - beam_max[:, None, :, None] - jnp.log(beam_total)[:, None, :, None]
        allowed_logprob = jnp.where(live_mask, shifted, 0.0)
        probabilities = jnp.where(live_mask, jnp.exp(shifted), 0.0).astype(jnp.bfloat16)

    prob_part = lax.all_gather(probabilities, "dp", axis=0, tiled=True)

    rows_per_dev = n_blk * BB // n_vocab
    pairs = BB // rows_per_dev // 2
    onehot = (
        block_lists[:, :, None] == jnp.arange(n_tb, dtype=jnp.int32)[None, None, :]
    ).astype(jnp.bfloat16)
    halves = prob_part.reshape(n_blk, MOST, pairs, 2, rows_per_dev, TB)
    low_bit = lax.axis_index("vocab") % 2

    def expected_half(which):
        with jax.named_scope("dense_expected"):
            chosen = lax.dynamic_index_in_dim(halves, which, axis=3, keepdims=False)
            chosen = chosen.reshape(n_blk, MOST, pairs * rows_per_dev, TB)
            spread = jnp.einsum(
                "bsk,bsrt->brkt", onehot, chosen, preferred_element_type=jnp.float32
            ).astype(jnp.bfloat16)
            term = jnp.einsum(
                "brkt,ktd->brd",
                spread,
                out_weight.reshape(n_tb, TB, columns_here),
                preferred_element_type=jnp.float32,
            )
            return term.reshape(n_blk * pairs, rows_per_dev, columns_here)

    send_half = expected_half(1 - low_bit)
    keep_half = expected_half(low_bit)
    summed = halving_reduce_scatter(keep_half, send_half, n_vocab)
    squares = butterfly_sum(jnp.sum(summed * summed, axis=1), "dp", n_dp)
    width = hidden.shape[1] * n_vocab
    expected = summed * lax.rsqrt(squares / width + 1e-06)[:, None]
    return (allowed_logprob[None], expected)


def solution(mesh):
    in_specs = (P("dp", "vocab"), P("vocab", "dp"), P("vocab", None, None), P("vocab", None))
    out_specs = (P("vocab", "dp", None, None, None), P("vocab", "dp"))
    return jax.shard_map(
        per_device, mesh=mesh, in_specs=in_specs, out_specs=out_specs, check_vma=False
    )
```

```python
import jax
import jax.numpy as jnp
from jax import lax
from jax.sharding import PartitionSpec as P

TB = 128
BB = 128
MOST = 16


def exchange_stage(x, remaining, bit, n):
    me = lax.axis_index("vocab")
    axis = remaining.index(bit)
    mine = (me // (1 << bit)) % 2
    keep = lax.dynamic_index_in_dim(x, mine, axis=axis, keepdims=False)
    send = lax.dynamic_index_in_dim(x, 1 - mine, axis=axis, keepdims=False)
    perm = [(s, s ^ (1 << bit)) for s in range(n)]
    got = lax.ppermute(send, "vocab", perm=perm)
    return keep + got, [b for b in remaining if b != bit]


def halving_reduce_scatter(keep, send, n):
    levels = n.bit_length() - 1
    _, group, cols = keep.shape
    perm = [(s, s ^ 1) for s in range(n)]
    half = cols // 2
    streams = []
    for cut in (slice(0, half), slice(half, cols)):
        with jax.named_scope("summed_core_stage"):
            x = keep[:, :, cut] + lax.ppermute(send[:, :, cut], "vocab", perm=perm)
        streams.append(x.reshape([2] * (levels - 1) + [group, half]))
    first, second = streams
    remaining = list(range(levels - 1, 0, -1))
    rest_a, rest_b = list(remaining), list(remaining)
    order_a = sorted(remaining)
    order_b = sorted(remaining, reverse=True)
    for step in range(len(order_a)):
        with jax.named_scope("summed_chip_stage"):
            first, rest_a = exchange_stage(first, rest_a, order_a[step], n)
            second, rest_b = exchange_stage(second, rest_b, order_b[step], n)
    return jnp.concatenate([first, second], axis=-1)


def gather_stage(x, have, bit, n):
    me = lax.axis_index("vocab")
    mine = (me // (1 << bit)) % 2
    perm = [(s, s ^ (1 << bit)) for s in range(n)]
    got = lax.ppermute(x, "vocab", perm=perm)
    pos = len([b for b in have if b > bit])
    low = jnp.stack([x, got], axis=pos)
    high = jnp.stack([got, x], axis=pos)
    return jnp.where(mine == 0, low, high), sorted(have + [bit], reverse=True)


def doubling_all_gather(x, n):
    levels = n.bit_length() - 1
    rows, cols = x.shape
    half = cols // 2
    first, second = x[:, :half], x[:, half:]
    have_a, have_b = [], []
    order_a = list(range(1, levels)) + [0]
    order_b = list(range(levels - 1, 0, -1)) + [0]
    for step in range(levels):
        with jax.named_scope("hidden_gather_stage"):
            first, have_a = gather_stage(first, have_a, order_a[step], n)
            second, have_b = gather_stage(second, have_b, order_b[step], n)
    joined = jnp.concatenate([first, second], axis=-1)
    return joined.reshape(n * rows, cols)


def butterfly_sum(x, axis_name, n):
    levels = n.bit_length() - 1
    for bit in range(levels):
        perm = [(s, s ^ (1 << bit)) for s in range(n)]
        x = x + lax.ppermute(x, axis_name, perm=perm)
    return x


def bruck_all_to_all(x, axis_name, n, split_axis, concat_axis):
    me = lax.axis_index(axis_name)
    levels = n.bit_length() - 1
    shape = list(x.shape)
    shape[split_axis : split_axis + 1] = [n, x.shape[split_axis] // n]
    pieces = jnp.moveaxis(x.reshape(shape), split_axis, 0)
    rest = pieces.shape[1:]
    held = pieces.reshape([2] * levels + list(rest))
    for bit in range(levels):
        pos = levels - 1 - bit
        mine = (me // (1 << bit)) % 2
        keep = lax.dynamic_index_in_dim(held, mine, axis=pos, keepdims=False)
        send = lax.dynamic_index_in_dim(held, 1 - mine, axis=pos, keepdims=False)
        perm = [(s, s ^ (1 << bit)) for s in range(n)]
        got = lax.ppermute(send, axis_name, perm=perm)
        low = jnp.stack([keep, got], axis=pos)
        high = jnp.stack([got, keep], axis=pos)
        held = jnp.where(mine == 0, low, high)
    by_source = held.reshape((n,) + tuple(rest))
    return jnp.concatenate([by_source[k] for k in range(n)], axis=concat_axis)


def per_device(hidden, out_weight, token_blocks, counts):
    vocab_here, columns_here = out_weight.shape
    n_vocab = lax.psum(1, "vocab")
    n_dp = lax.psum(1, "dp")
    n_tb = vocab_here // TB
    block_lists = token_blocks[0]
    block_counts = counts[0]
    n_blk = block_lists.shape[0]
    own_blocks = hidden.shape[0] // BB
    assert own_blocks == 1 and n_blk == n_dp
    me_dp = lax.axis_index("dp")
    own_counts = lax.dynamic_slice_in_dim(block_counts, me_dp, 1, 0)

    with jax.named_scope("hidden_spread"):
        row_slices = bruck_all_to_all(hidden, "vocab", n_vocab, split_axis=0, concat_axis=1)
        plane_rows = bruck_all_to_all(row_slices, "dp", n_dp, split_axis=1, concat_axis=0)
        gathered = doubling_all_gather(plane_rows, n_vocab)
        group = hidden.shape[0] // n_vocab
        beam_columns = (
            gathered.reshape(n_vocab, n_dp, group, columns_here)
            .transpose(1, 0, 2, 3)
            .reshape(n_dp * n_vocab * group, columns_here)
        )

    with jax.named_scope("dense_logits"):
        full = jnp.einsum(
            "bd,vd->bv", beam_columns, out_weight, preferred_element_type=jnp.float32
        )
        full4 = full.reshape(n_blk, BB, n_tb, TB)
        rows = jnp.arange(n_blk, dtype=jnp.int32)[:, None]
        picked = full4[rows, :, block_lists, :]

    logits = lax.psum_scatter(picked, "dp", scatter_dimension=0, tiled=True)

    with jax.named_scope("softmax_stats"):
        live = jnp.arange(MOST, dtype=jnp.int32)[None, :] < own_counts[:, None]
        live_mask = live[:, :, None, None]
        masked = jnp.where(live_mask, logits, -jnp.inf)
        local_max = jnp.max(masked, axis=(1, 3))
        local_total = jnp.sum(jnp.exp(masked - local_max[:, None, :, None]), axis=(1, 3))
        stats = lax.all_gather(jnp.stack([local_max, local_total]), "vocab", axis=0)
        beam_max = jnp.max(stats[:, 0], axis=0)
        beam_total = jnp.sum(stats[:, 1] * jnp.exp(stats[:, 0] - beam_max[None]), axis=0)
        shifted = logits - beam_max[:, None, :, None] - jnp.log(beam_total)[:, None, :, None]
        probabilities = jnp.where(live_mask, jnp.exp(shifted), 0.0).astype(jnp.bfloat16)
        later, probabilities = lax.optimization_barrier((shifted, probabilities))
        allowed_logprob = jnp.where(live_mask, later, 0.0)

    prob_part = lax.all_gather(probabilities, "dp", axis=0, tiled=True)

    rows_per_dev = n_blk * BB // n_vocab
    pairs = BB // rows_per_dev // 2
    onehot = (
        block_lists[:, :, None] == jnp.arange(n_tb, dtype=jnp.int32)[None, None, :]
    ).astype(jnp.bfloat16)
    halves = prob_part.reshape(n_blk, MOST, pairs, 2, rows_per_dev, TB)
    low_bit = lax.axis_index("vocab") % 2

    def expected_half(which):
        with jax.named_scope("dense_expected"):
            chosen = lax.dynamic_index_in_dim(halves, which, axis=3, keepdims=False)
            chosen = chosen.reshape(n_blk, MOST, pairs * rows_per_dev, TB)
            spread = jnp.einsum(
                "bsk,bsrt->brkt", onehot, chosen, preferred_element_type=jnp.float32
            ).astype(jnp.bfloat16)
            term = jnp.einsum(
                "brkt,ktd->brd",
                spread,
                out_weight.reshape(n_tb, TB, columns_here),
                preferred_element_type=jnp.float32,
            )
            return term.reshape(n_blk * pairs, rows_per_dev, columns_here)

    send_half = expected_half(1 - low_bit)
    keep_half = expected_half(low_bit)
    summed = halving_reduce_scatter(keep_half, send_half, n_vocab)
    squares = butterfly_sum(jnp.sum(summed * summed, axis=1), "dp", n_dp)
    width = hidden.shape[1] * n_vocab
    expected = summed * lax.rsqrt(squares / width + 1e-06)[:, None]
    return (allowed_logprob[None], expected)


def solution(mesh):
    in_specs = (P("dp", "vocab"), P("vocab", "dp"), P("vocab", None, None), P("vocab", None))
    out_specs = (P("vocab", "dp", None, None, None), P("vocab", "dp"))
    return jax.shard_map(
        per_device, mesh=mesh, in_specs=in_specs, out_specs=out_specs, check_vma=False
    )
```

```python
import jax
import jax.numpy as jnp
from jax import lax
from jax.sharding import PartitionSpec as P

TB = 128
BB = 128
MOST = 16


def exchange_stage(x, remaining, bit, n):
    me = lax.axis_index("vocab")
    axis = remaining.index(bit)
    mine = (me // (1 << bit)) % 2
    keep = lax.dynamic_index_in_dim(x, mine, axis=axis, keepdims=False)
    send = lax.dynamic_index_in_dim(x, 1 - mine, axis=axis, keepdims=False)
    perm = [(s, s ^ (1 << bit)) for s in range(n)]
    got = lax.ppermute(send, "vocab", perm=perm)
    return keep + got, [b for b in remaining if b != bit]


def halving_reduce_scatter(keep, send, n):
    levels = n.bit_length() - 1
    _, group, cols = keep.shape
    perm = [(s, s ^ 1) for s in range(n)]
    half = cols // 2
    streams = []
    for cut in (slice(0, half), slice(half, cols)):
        with jax.named_scope("summed_core_stage"):
            x = keep[:, :, cut] + lax.ppermute(send[:, :, cut], "vocab", perm=perm)
        streams.append(x.reshape([2] * (levels - 1) + [group, half]))
    first, second = streams
    remaining = list(range(levels - 1, 0, -1))
    rest_a, rest_b = list(remaining), list(remaining)
    order_a = sorted(remaining)
    order_b = sorted(remaining, reverse=True)
    for step in range(len(order_a)):
        with jax.named_scope("summed_chip_stage"):
            first, rest_a = exchange_stage(first, rest_a, order_a[step], n)
            second, rest_b = exchange_stage(second, rest_b, order_b[step], n)
    return jnp.concatenate([first, second], axis=-1)


def gather_stage(x, have, bit, n):
    me = lax.axis_index("vocab")
    mine = (me // (1 << bit)) % 2
    perm = [(s, s ^ (1 << bit)) for s in range(n)]
    got = lax.ppermute(x, "vocab", perm=perm)
    pos = len([b for b in have if b > bit])
    low = jnp.stack([x, got], axis=pos)
    high = jnp.stack([got, x], axis=pos)
    return jnp.where(mine == 0, low, high), sorted(have + [bit], reverse=True)


def doubling_all_gather(x, n):
    levels = n.bit_length() - 1
    rows, cols = x.shape
    half = cols // 2
    first, second = x[:, :half], x[:, half:]
    have_a, have_b = [], []
    order_a = list(range(1, levels)) + [0]
    order_b = list(range(levels - 1, 0, -1)) + [0]
    for step in range(levels):
        with jax.named_scope("hidden_gather_stage"):
            first, have_a = gather_stage(first, have_a, order_a[step], n)
            second, have_b = gather_stage(second, have_b, order_b[step], n)
    joined = jnp.concatenate([first, second], axis=-1)
    return joined.reshape(n * rows, cols)


def butterfly_sum(x, axis_name, n):
    levels = n.bit_length() - 1
    for bit in range(levels):
        perm = [(s, s ^ (1 << bit)) for s in range(n)]
        x = x + lax.ppermute(x, axis_name, perm=perm)
    return x


def bruck_all_to_all(x, axis_name, n, split_axis, concat_axis):
    me = lax.axis_index(axis_name)
    levels = n.bit_length() - 1
    shape = list(x.shape)
    shape[split_axis : split_axis + 1] = [n, x.shape[split_axis] // n]
    pieces = jnp.moveaxis(x.reshape(shape), split_axis, 0)
    rest = pieces.shape[1:]
    held = pieces.reshape([2] * levels + list(rest))
    for bit in range(levels):
        pos = levels - 1 - bit
        mine = (me // (1 << bit)) % 2
        keep = lax.dynamic_index_in_dim(held, mine, axis=pos, keepdims=False)
        send = lax.dynamic_index_in_dim(held, 1 - mine, axis=pos, keepdims=False)
        perm = [(s, s ^ (1 << bit)) for s in range(n)]
        got = lax.ppermute(send, axis_name, perm=perm)
        low = jnp.stack([keep, got], axis=pos)
        high = jnp.stack([got, keep], axis=pos)
        held = jnp.where(mine == 0, low, high)
    by_source = held.reshape((n,) + tuple(rest))
    return jnp.concatenate([by_source[k] for k in range(n)], axis=concat_axis)


def per_device(hidden, out_weight, token_blocks, counts):
    vocab_here, columns_here = out_weight.shape
    n_vocab = lax.psum(1, "vocab")
    n_dp = lax.psum(1, "dp")
    n_tb = vocab_here // TB
    block_lists = token_blocks[0]
    block_counts = counts[0]
    n_blk = block_lists.shape[0]
    own_blocks = hidden.shape[0] // BB
    assert own_blocks == 1 and n_blk == n_dp
    me_dp = lax.axis_index("dp")
    own_counts = lax.dynamic_slice_in_dim(block_counts, me_dp, 1, 0)

    with jax.named_scope("hidden_spread"):
        row_slices = bruck_all_to_all(hidden, "vocab", n_vocab, split_axis=0, concat_axis=1)
        plane_rows = bruck_all_to_all(row_slices, "dp", n_dp, split_axis=1, concat_axis=0)
        gathered = doubling_all_gather(plane_rows, n_vocab)
        group = hidden.shape[0] // n_vocab
        beam_columns = (
            gathered.reshape(n_vocab, n_dp, group, columns_here)
            .transpose(1, 0, 2, 3)
            .reshape(n_dp * n_vocab * group, columns_here)
        )

    with jax.named_scope("dense_logits"):
        full = jnp.einsum(
            "bd,vd->bv", beam_columns, out_weight, preferred_element_type=jnp.float32
        )
        full4 = full.reshape(n_blk, BB, n_tb, TB)
        rows = jnp.arange(n_blk, dtype=jnp.int32)[:, None]
        picked = full4[rows, :, block_lists, :]

    logits = lax.psum_scatter(picked, "dp", scatter_dimension=0, tiled=True)

    with jax.named_scope("softmax_stats"):
        live = jnp.arange(MOST, dtype=jnp.int32)[None, :] < own_counts[:, None]
        live_mask = live[:, :, None, None]
        masked = jnp.where(live_mask, logits, -jnp.inf)
        local_max = jnp.max(masked, axis=(1, 3))
        local_total = jnp.sum(jnp.exp(masked - local_max[:, None, :, None]), axis=(1, 3))
        stats = lax.all_gather(jnp.stack([local_max, local_total]), "vocab", axis=0)
        beam_max = jnp.max(stats[:, 0], axis=0)
        beam_total = jnp.sum(stats[:, 1] * jnp.exp(stats[:, 0] - beam_max[None]), axis=0)
        shifted = logits - beam_max[:, None, :, None] - jnp.log(beam_total)[:, None, :, None]
        probabilities = jnp.where(live_mask, jnp.exp(shifted), 0.0).astype(jnp.bfloat16)
        later, probabilities = lax.optimization_barrier((shifted, probabilities))
        allowed_logprob = jnp.where(live_mask, later, 0.0)

    rows_per_dev = n_blk * BB // n_vocab
    pairs = BB // rows_per_dev // 2
    split_rows = probabilities.reshape(1, MOST, pairs, 2, rows_per_dev, TB)
    send_first = jnp.where(
        lax.axis_index("vocab") % 2 == 0, jnp.flip(split_rows, axis=3), split_rows
    ).reshape(probabilities.shape)
    prob_part = lax.all_gather(send_first, "dp", axis=0, tiled=True)

    rows_per_dev = n_blk * BB // n_vocab
    pairs = BB // rows_per_dev // 2
    onehot = (
        block_lists[:, :, None] == jnp.arange(n_tb, dtype=jnp.int32)[None, None, :]
    ).astype(jnp.bfloat16)
    halves = prob_part.reshape(n_blk, MOST, pairs, 2, rows_per_dev, TB)
    low_bit = lax.axis_index("vocab") % 2

    def expected_half(which):
        with jax.named_scope("dense_expected"):
            chosen = halves[:, :, :, which]
            chosen = chosen.reshape(n_blk, MOST, pairs * rows_per_dev, TB)
            spread = jnp.einsum(
                "bsk,bsrt->brkt", onehot, chosen, preferred_element_type=jnp.float32
            ).astype(jnp.bfloat16)
            term = jnp.einsum(
                "brkt,ktd->brd",
                spread,
                out_weight.reshape(n_tb, TB, columns_here),
                preferred_element_type=jnp.float32,
            )
            return term.reshape(n_blk * pairs, rows_per_dev, columns_here)

    send_half = expected_half(0)
    keep_half = expected_half(1)
    summed = halving_reduce_scatter(keep_half, send_half, n_vocab)
    squares = butterfly_sum(jnp.sum(summed * summed, axis=1), "dp", n_dp)
    width = hidden.shape[1] * n_vocab
    expected = summed * lax.rsqrt(squares / width + 1e-06)[:, None]
    return (allowed_logprob[None], expected)


def solution(mesh):
    in_specs = (P("dp", "vocab"), P("vocab", "dp"), P("vocab", None, None), P("vocab", None))
    out_specs = (P("vocab", "dp", None, None, None), P("vocab", "dp"))
    return jax.shard_map(
        per_device, mesh=mesh, in_specs=in_specs, out_specs=out_specs, check_vma=False
    )
```

```python
import jax
import jax.numpy as jnp
from jax import lax
from jax.sharding import PartitionSpec as P

TB = 128
BB = 128
MOST = 16


def exchange_stage(x, remaining, bit, n):
    me = lax.axis_index("vocab")
    axis = remaining.index(bit)
    mine = (me // (1 << bit)) % 2
    keep = lax.dynamic_index_in_dim(x, mine, axis=axis, keepdims=False)
    send = lax.dynamic_index_in_dim(x, 1 - mine, axis=axis, keepdims=False)
    perm = [(s, s ^ (1 << bit)) for s in range(n)]
    got = lax.ppermute(send, "vocab", perm=perm)
    return keep + got, [b for b in remaining if b != bit]


def halving_reduce_scatter(keep, send, n):
    levels = n.bit_length() - 1
    _, group, cols = keep.shape
    perm = [(s, s ^ 1) for s in range(n)]
    half = cols // 2
    streams = []
    for cut in (slice(0, half), slice(half, cols)):
        with jax.named_scope("summed_core_stage"):
            x = keep[:, :, cut] + lax.ppermute(send[:, :, cut], "vocab", perm=perm)
        streams.append(x.reshape([2] * (levels - 1) + [group, half]))
    first, second = streams
    remaining = list(range(levels - 1, 0, -1))
    rest_a, rest_b = list(remaining), list(remaining)
    order_a = sorted(remaining)
    order_b = sorted(remaining, reverse=True)
    for step in range(len(order_a)):
        with jax.named_scope("summed_chip_stage"):
            first, rest_a = exchange_stage(first, rest_a, order_a[step], n)
            second, rest_b = exchange_stage(second, rest_b, order_b[step], n)
    return jnp.concatenate([first, second], axis=-1)


def gather_stage(x, have, bit, n):
    me = lax.axis_index("vocab")
    mine = (me // (1 << bit)) % 2
    perm = [(s, s ^ (1 << bit)) for s in range(n)]
    got = lax.ppermute(x, "vocab", perm=perm)
    pos = len([b for b in have if b > bit])
    low = jnp.stack([x, got], axis=pos)
    high = jnp.stack([got, x], axis=pos)
    return jnp.where(mine == 0, low, high), sorted(have + [bit], reverse=True)


def doubling_all_gather(x, n):
    levels = n.bit_length() - 1
    rows, cols = x.shape
    half = cols // 2
    first, second = x[:, :half], x[:, half:]
    have_a, have_b = [], []
    order_a = list(range(1, levels)) + [0]
    order_b = list(range(levels - 1, 0, -1)) + [0]
    for step in range(levels):
        with jax.named_scope("hidden_gather_stage"):
            first, have_a = gather_stage(first, have_a, order_a[step], n)
            second, have_b = gather_stage(second, have_b, order_b[step], n)
    joined = jnp.concatenate([first, second], axis=-1)
    return joined.reshape(n * rows, cols)


def butterfly_sum(x, axis_name, n):
    levels = n.bit_length() - 1
    for bit in range(levels):
        perm = [(s, s ^ (1 << bit)) for s in range(n)]
        x = x + lax.ppermute(x, axis_name, perm=perm)
    return x


def bruck_all_to_all(x, axis_name, n, split_axis, concat_axis):
    me = lax.axis_index(axis_name)
    levels = n.bit_length() - 1
    shape = list(x.shape)
    shape[split_axis : split_axis + 1] = [n, x.shape[split_axis] // n]
    pieces = jnp.moveaxis(x.reshape(shape), split_axis, 0)
    rest = pieces.shape[1:]
    held = pieces.reshape([2] * levels + list(rest))
    for bit in range(levels):
        pos = levels - 1 - bit
        mine = (me // (1 << bit)) % 2
        keep = lax.dynamic_index_in_dim(held, mine, axis=pos, keepdims=False)
        send = lax.dynamic_index_in_dim(held, 1 - mine, axis=pos, keepdims=False)
        perm = [(s, s ^ (1 << bit)) for s in range(n)]
        got = lax.ppermute(send, axis_name, perm=perm)
        low = jnp.stack([keep, got], axis=pos)
        high = jnp.stack([got, keep], axis=pos)
        held = jnp.where(mine == 0, low, high)
    by_source = held.reshape((n,) + tuple(rest))
    return jnp.concatenate([by_source[k] for k in range(n)], axis=concat_axis)


def direct_spread(hidden, n_vocab, n_dp):
    rows, chunk = hidden.shape
    per_slice = n_vocab // n_dp
    group = rows // n_vocab
    me_v = lax.axis_index("vocab")
    me_d = lax.axis_index("dp")
    pieces = hidden.reshape(n_vocab, group, chunk)
    got = []
    for shift in range(n_vocab):
        target = (me_v % per_slice + per_slice * me_d + shift) % n_vocab
        send = lax.dynamic_index_in_dim(pieces, target, axis=0, keepdims=False)
        perm = []
        for d in range(n_dp):
            for v in range(n_vocab):
                k = (v % per_slice + per_slice * d + shift) % n_vocab
                perm.append((d * n_vocab + v, (v // per_slice) * n_vocab + k))
        got.append(lax.ppermute(send, ("dp", "vocab"), perm=perm))
    received = jnp.stack(got)
    slot = jnp.arange(n_vocab, dtype=jnp.int32)
    order = (me_v - slot) % n_vocab
    placed = jnp.take(received, order, axis=0)
    placed = placed.reshape(n_dp, per_slice, group, chunk).transpose(0, 2, 1, 3)
    return placed.reshape(n_dp * group, per_slice * chunk)


def per_device(hidden, out_weight, token_blocks, counts):
    vocab_here, columns_here = out_weight.shape
    n_vocab = lax.psum(1, "vocab")
    n_dp = lax.psum(1, "dp")
    n_tb = vocab_here // TB
    block_lists = token_blocks[0]
    block_counts = counts[0]
    n_blk = block_lists.shape[0]
    own_blocks = hidden.shape[0] // BB
    assert own_blocks == 1 and n_blk == n_dp
    me_dp = lax.axis_index("dp")
    own_counts = lax.dynamic_slice_in_dim(block_counts, me_dp, 1, 0)

    with jax.named_scope("hidden_spread"):
        plane_rows = direct_spread(hidden, n_vocab, n_dp)
        gathered = doubling_all_gather(plane_rows, n_vocab)
        group = hidden.shape[0] // n_vocab
        beam_columns = (
            gathered.reshape(n_vocab, n_dp, group, columns_here)
            .transpose(1, 0, 2, 3)
            .reshape(n_dp * n_vocab * group, columns_here)
        )

    with jax.named_scope("dense_logits"):
        full = jnp.einsum(
            "bd,vd->bv", beam_columns, out_weight, preferred_element_type=jnp.float32
        )
        full4 = full.reshape(n_blk, BB, n_tb, TB)
        rows = jnp.arange(n_blk, dtype=jnp.int32)[:, None]
        picked = full4[rows, :, block_lists, :]

    logits = lax.psum_scatter(picked, "dp", scatter_dimension=0, tiled=True)

    with jax.named_scope("softmax_stats"):
        live = jnp.arange(MOST, dtype=jnp.int32)[None, :] < own_counts[:, None]
        live_mask = live[:, :, None, None]
        masked = jnp.where(live_mask, logits, -jnp.inf)
        local_max = jnp.max(masked, axis=(1, 3))
        local_total = jnp.sum(jnp.exp(masked - local_max[:, None, :, None]), axis=(1, 3))
        stats = lax.all_gather(jnp.stack([local_max, local_total]), "vocab", axis=0)
        beam_max = jnp.max(stats[:, 0], axis=0)
        beam_total = jnp.sum(stats[:, 1] * jnp.exp(stats[:, 0] - beam_max[None]), axis=0)
        shifted = logits - beam_max[:, None, :, None] - jnp.log(beam_total)[:, None, :, None]
        probabilities = jnp.where(live_mask, jnp.exp(shifted), 0.0).astype(jnp.bfloat16)
        later, probabilities = lax.optimization_barrier((shifted, probabilities))
        allowed_logprob = jnp.where(live_mask, later, 0.0)

    prob_part = lax.all_gather(probabilities, "dp", axis=0, tiled=True)

    rows_per_dev = n_blk * BB // n_vocab
    pairs = BB // rows_per_dev // 2
    onehot = (
        block_lists[:, :, None] == jnp.arange(n_tb, dtype=jnp.int32)[None, None, :]
    ).astype(jnp.bfloat16)
    halves = prob_part.reshape(n_blk, MOST, pairs, 2, rows_per_dev, TB)
    low_bit = lax.axis_index("vocab") % 2

    def expected_half(which):
        with jax.named_scope("dense_expected"):
            chosen = lax.dynamic_index_in_dim(halves, which, axis=3, keepdims=False)
            chosen = chosen.reshape(n_blk, MOST, pairs * rows_per_dev, TB)
            spread = jnp.einsum(
                "bsk,bsrt->brkt", onehot, chosen, preferred_element_type=jnp.float32
            ).astype(jnp.bfloat16)
            term = jnp.einsum(
                "brkt,ktd->brd",
                spread,
                out_weight.reshape(n_tb, TB, columns_here),
                preferred_element_type=jnp.float32,
            )
            return term.reshape(n_blk * pairs, rows_per_dev, columns_here)

    send_half = expected_half(1 - low_bit)
    keep_half = expected_half(low_bit)
    summed = halving_reduce_scatter(keep_half, send_half, n_vocab)
    squares = butterfly_sum(jnp.sum(summed * summed, axis=1), "dp", n_dp)
    width = hidden.shape[1] * n_vocab
    expected = summed * lax.rsqrt(squares / width + 1e-06)[:, None]
    return (allowed_logprob[None], expected)


def solution(mesh):
    in_specs = (P("dp", "vocab"), P("vocab", "dp"), P("vocab", None, None), P("vocab", None))
    out_specs = (P("vocab", "dp", None, None, None), P("vocab", "dp"))
    return jax.shard_map(
        per_device, mesh=mesh, in_specs=in_specs, out_specs=out_specs, check_vma=False
    )
```
